128 devices in a mesh: req: 16 (over z, y), cuts: 8 (over x, core).
Axes of the slice: x: 4, y: 4, z: 4, core: 2. Of those that a mesh axis runs over, the one named last changes fastest.
Arguments:
- tokens: bfloat16 [16384, 1024], P(('req', 'cuts')), may hold values from -6 to 6
- qkv_weight: bfloat16 [1024, 2048], replicated, may hold values from -0.1875 to 0.1875
- out_weight: bfloat16 [1024, 1024], replicated, may hold values from -0.1875 to 0.1875
- norm_attn: float32 [1024], replicated, may hold values from 0.4 to 1.6
- norm_expert: float32 [1024], replicated, may hold values from 0.4 to 1.6
- keys_cache: bfloat16 [128, 2048, 512], P(('req', 'cuts')), may hold values from -4000 to 4000
- values_cache: bfloat16 [128, 2048, 512], P(('req', 'cuts')), may hold values from -6 to 6
- lengths: int32 [128], P(('req', 'cuts')), may hold values from 1 to 2048, 131072 in all
- routes: int32 [16384, 8], P(('req', 'cuts')), may hold values from 0 to 31, all different within a row; in each aligned block of 128 rows (0 to 127, 128 to 255, ...) at most 40 rows name the same one
- gates: float32 [16384, 8], P(('req', 'cuts')), may hold values from 0.05 to 0.25
- gate_up: bfloat16 [128, 1024, 256], P(('req', 'cuts')), may hold values from -0.1875 to 0.1875
- down_weight: bfloat16 [128, 128, 1024], P(('req', 'cuts')), may hold values from -0.25 to 0.25
Outputs:
- attn_branch: bfloat16 [16384, 1024], P(('req', 'cuts'))
- expert_mix: bfloat16 [16384, 1024], P(('req', 'cuts'))
The draws below stay inside these ranges and needn't reach their ends.
Inputs may be any that keep to these rules, and one draw needn't show every extreme that they name: `routes`: each row names 8 different experts; within the 128 rows of one request no expert is named by more than 40 rows, a bound that some block reaches. `lengths`: one request has exactly 2048 live cache slots.
All inputs are finite; a program needn't handle non-finite values. No bound on the sum of `lengths` on one device may be relied on, other than what follows from the above.
Results may differ from the reference program's by a relative error of at most 0.012.
The reference program's roundings to bfloat16 on the way count: a program that leaves them out, or rounds other values in their place, can miss the bound.
Values may be sent and summed in bfloat16 or wider, within the bound.
No kernel may reach another device: no remote copies, remote signals or barrier semaphores. Data moves between devices by JAX's collectives and lax.ppermute only.
A program may use at most 128 MiB of HBM per device.

```python
import math
import jax
import jax.numpy as jnp
import numpy as np
from jax import lax

D = 1024
HEADS = 16
KV_HEADS = 8
HEAD = 64
EXPERTS = 32
HID = 512
TOP = 8
STRETCH = 128
CAP = 2048
REQS = 128
TOKENS = 16384
QW = 1024
KVW = 512
SLICES = 4
HID_DEV = 128
CAPACITY = 40
DEVICES = 128


def draw_keys_cache(key, part):
    first = jax.random.fold_in(key, 0)
    base = 16.0 * jnp.clip(jax.random.normal(first, (REQS, CAP, KV_HEADS * HEAD), jnp.float32), -6.0, 6.0)
    return base.astype(jnp.bfloat16)


def shard_levels(own_key, extent, pieces, smallest, largest):
    factor_of = 1.0
    for axis_at, blocks in pieces:
        heights = jax.random.uniform(jax.random.fold_in(jax.random.fold_in(own_key, 6), axis_at), (blocks,), jnp.float32, smallest / len(pieces), largest / len(pieces))
        factor_of = factor_of * jnp.repeat(jnp.exp(heights), extent[axis_at] // blocks).reshape((-1,) + (1,) * (len(extent) - 1 - axis_at))
    return factor_of


def profile(number_of, total, most, skew):
    loads = [(1 << 20) // math.isqrt(grade ** skew) + 1 for grade in range(2, number_of + 1)]
    surplus, counts = total - most - (number_of - 1), [1] * (number_of - 1)
    while surplus > 0:
        candidates = [i for i in range(number_of - 1) if counts[i] < most]
        mass, budget = sum([loads[i] for i in candidates]), surplus
        for i in candidates:
            addition = min(most - counts[i], max(1, budget * loads[i] // mass), surplus)
            counts[i] = counts[i] + addition
            surplus = surplus - addition
    return np.array([most] + counts)


def ragged_sizes(key, number_of, total, limit, slope):
    if number_of == 2:
        one = jax.random.randint(key, (), max(1, total - limit), min(limit, total - 1) + 1)
        return jnp.stack([one, total - one])
    tallies = jnp.asarray(profile(number_of, total, limit, slope), jnp.int32)
    pairs = (number_of - 1) // 2
    source_of, sink = tallies[1:1 + 2 * pairs:2], tallies[2:2 + 2 * pairs:2]
    slack = jnp.minimum(source_of - 1, limit - sink)
    passed = jax.random.randint(jax.random.fold_in(key, 1), (pairs,), 0, 1 << 20) % (slack + 1)
    tallies = tallies.at[1:1 + 2 * pairs:2].set(source_of - passed).at[2:2 + 2 * pairs:2].set(sink + passed)
    return tallies[jax.random.permutation(jax.random.fold_in(key, 2), number_of)]


def deal_out(rng, own, number, rows, number_of, top, most, lean):
    sequence = jax.random.permutation(rng, number_of)
    crowded, common = portions_of(number_of, rows * top, most, lean, True), portions_of(number_of, rows * top, most, lean, False)
    places = jnp.arange(number_of)

    def named(sizes, offset_by):
        used = int((sizes > 0).sum())
        fixed = max(1, used // 4)
        shifted = fixed + (places - fixed + offset_by * (used - fixed)) % max(1, number_of - fixed)
        return jnp.zeros((number_of,), jnp.int32).at[sequence[jnp.where(places < fixed, places, shifted)]].set(jnp.asarray(sizes, jnp.int32))

    sizes = jnp.where(number % 4 == 0, named(crowded, number // 4), named(common, number - number // 4 - 1))
    mixed = jax.random.permutation(jax.random.fold_in(own, 3), number_of)
    source_of, sink = mixed[0:number_of // 2 * 2:2], mixed[1:number_of // 2 * 2:2]
    slack = jnp.minimum(sizes[source_of] - 1, most - sizes[sink]) // 2
    slack = jnp.where((source_of == sequence[0]) | (sink == sequence[0]) | (sizes[sink] == 0), 0, jnp.maximum(slack, 0))
    shifted = jax.random.randint(jax.random.fold_in(own, 4), (number_of // 2,), 0, 1 << 20) % (slack + 1)
    sizes = sizes.at[source_of].add(-shifted).at[sink].add(shifted)
    items = jnp.searchsorted(jnp.cumsum(sizes), jnp.arange(rows * top), side="right").astype(jnp.int32)
    grid = items.reshape(top, rows).T
    grid = grid[jax.random.permutation(jax.random.fold_in(own, 1), rows)]
    offset_by = jax.random.randint(jax.random.fold_in(own, 2), (rows, 1), 0, top)
    return jnp.take_along_axis(grid, (jnp.arange(top)[None, :] + offset_by) % top, axis=1)


def portions_of(number_of, total, limit, skew, full):
    portions = [(1 << 20) // math.isqrt(rank ** skew) + 1 for rank in range(1, number_of + 1)]
    largest = limit if full else min(limit, max(-(-total // number_of), total * portions[0] // sum(portions)))
    least = 1 if total - largest >= number_of - 1 else 0
    holding, rest = [largest] + [least] * (number_of - 1), total - largest - least * (number_of - 1)
    while rest > 0:
        free = [i for i in range(1, number_of) if holding[i] < largest] or [i for i in range(1, number_of) if holding[i] < limit]
        whole, budget = sum([portions[i] for i in free]), rest
        for i in free:
            more = min(limit - holding[i], max(1, budget * portions[i] // whole), rest)
            holding[i] = holding[i] + more
            rest = rest - more
    return np.array(holding)


def gaussian(key, dims, width, limit, cuts=(), held_as=jnp.bfloat16):
    drawn = jax.random.normal(key, dims, jnp.float32) * width
    if len(cuts) > 0:
        drawn = shard_levels(key, dims, cuts, -0.22, 0.18) * drawn
    return jnp.clip(drawn, min=-limit, max=limit).astype(held_as)


def setup_inputs(seed: int = 0) -> dict:
    key_list = jax.random.split(jax.random.key(seed), 13)
    tokens = gaussian(key_list[0], (TOKENS, D), 1.0, 6.0, ((0, 128),))
    qkv_weight = gaussian(key_list[1], (D, QW + 2 * KVW), D ** -0.5, 0.1875)
    out_weight = gaussian(key_list[2], (QW, D), QW ** -0.5, 0.1875)
    norm_attn = jnp.clip(1.0 + 0.12 * jax.random.normal(key_list[3], (D,), jnp.float32), 0.4, 1.6)
    norm_expert = jnp.clip(1.0 + 0.12 * jax.random.normal(key_list[4], (D,), jnp.float32), 0.4, 1.6)
    keys_cache = draw_keys_cache(jax.random.fold_in(key_list[12], 71), 0)
    values_cache = gaussian(key_list[6], (REQS, CAP, KVW), 1.0, 6.0, ((0, 128),))
    lengths = ragged_sizes(key_list[7], REQS, REQS * CAP // 2, CAP, 2).astype(jnp.int32)
    routes_keys = jax.random.split(jax.random.fold_in(key_list[8], 1), TOKENS // STRETCH)
    routes_turns = jax.random.permutation(jax.random.fold_in(key_list[8], 3), TOKENS // STRETCH)
    routes = jax.vmap(lambda own, number: deal_out(jax.random.fold_in(key_list[8], 2), own, number, STRETCH, EXPERTS, TOP, CAPACITY, 2))(routes_keys, routes_turns).reshape((TOKENS, TOP))
    gates = jnp.clip(0.05 + 0.2 * jax.random.uniform(key_list[9], (TOKENS, TOP), jnp.float32) ** shard_levels(key_list[9], (TOKENS, TOP), ((0, 128),), -0.2, 0.2), 0.05, 0.25)
    gate_up = gaussian(key_list[10], (DEVICES, D, 2 * HID_DEV), D ** -0.5, 0.1875, ((0, 128),))
    down_weight = gaussian(key_list[11], (DEVICES, HID_DEV, D), HID ** -0.5, 0.25, ((0, 128),))
    return {"tokens": tokens, "qkv_weight": qkv_weight, "out_weight": out_weight, "norm_attn": norm_attn, "norm_expert": norm_expert, "keys_cache": keys_cache, "values_cache": values_cache, "lengths": lengths, "routes": routes, "gates": gates, "gate_up": gate_up, "down_weight": down_weight}


def rms_scale(values, gain):
    wide = values.astype(jnp.float32)
    power = lax.optimization_barrier(jnp.mean(wide * wide, axis=-1, keepdims=True))
    return wide * lax.rsqrt(power + 1e-06) * gain

def rotate(vectors, places):
    half = vectors.shape[-1] // 2
    freq = 10000.0 ** (-jnp.arange(half, dtype=jnp.float32) / half)
    angle = places[:, None] * freq[None, :]
    cosine = jnp.cos(angle)[:, None, :]
    sine = jnp.sin(angle)[:, None, :]
    first = vectors[..., :half]
    second = vectors[..., half:]
    return jnp.concatenate([first * cosine - second * sine, second * cosine + first * sine], axis=-1)

def attend(tokens, qkv_weight, out_weight, norm_attn, keys_cache, values_cache, length):
    rows = tokens.shape[0]
    span = keys_cache.shape[0]
    qwidth = HEADS * HEAD
    kvwidth = KV_HEADS * HEAD
    normed = rms_scale(tokens, norm_attn).astype(jnp.bfloat16)
    mixed = jnp.dot(normed, qkv_weight, preferred_element_type=jnp.float32)
    places = (length + jnp.arange(rows, dtype=jnp.int32)).astype(jnp.float32)
    query = rotate(mixed[:, :qwidth].reshape(rows, HEADS, HEAD), places).astype(jnp.bfloat16)
    key_new = rotate(mixed[:, qwidth:qwidth + kvwidth].reshape(rows, KV_HEADS, HEAD), places).astype(jnp.bfloat16)
    value_new = mixed[:, qwidth + kvwidth:].astype(jnp.bfloat16)
    keys = jnp.concatenate([keys_cache, key_new.reshape(rows, kvwidth)], axis=0).reshape(span + rows, KV_HEADS, HEAD)
    values = jnp.concatenate([values_cache, value_new], axis=0).reshape(span + rows, KV_HEADS, HEAD)
    query = query.reshape(rows, KV_HEADS, HEADS // KV_HEADS, HEAD)
    scores = jnp.einsum('tkgd,skd->kgts', query.astype(jnp.float32), keys.astype(jnp.float32)) * 0.015625
    column = jnp.arange(span + rows, dtype=jnp.int32)[None, :]
    row_index = jnp.arange(rows, dtype=jnp.int32)[:, None]
    valid = jnp.where(column < span, column < length, column - span <= row_index)
    scores = jnp.where(valid[None, None], scores, -1e+30)
    top = lax.optimization_barrier(jnp.max(scores, axis=-1, keepdims=True))
    weights = jnp.exp(scores - top)
    weights = (weights / lax.optimization_barrier(jnp.sum(weights, axis=-1, keepdims=True))).astype(jnp.bfloat16)
    heads_out = jnp.einsum('kgts,skd->tkgd', weights.astype(jnp.float32), values.astype(jnp.float32))
    heads_out = heads_out.astype(jnp.bfloat16).reshape(rows, qwidth)
    return jnp.dot(heads_out, out_weight, preferred_element_type=jnp.float32)

def reference(tokens, qkv_weight, out_weight, norm_attn, norm_expert, keys_cache, values_cache, lengths, routes, gates, gate_up, down_weight):
    stretches = tokens.reshape(REQS, STRETCH, D)

    def one_request(items):
        piece, key_rows, value_rows, length = items
        return attend(piece, qkv_weight, out_weight, norm_attn, key_rows, value_rows, length)
    branch = lax.map(one_request, (stretches, keys_cache, values_cache, lengths)).reshape(TOKENS, D)
    carried = tokens.astype(jnp.float32) + 0.22 * branch
    normed = rms_scale(carried, norm_expert).astype(jnp.bfloat16)
    padded = jnp.concatenate([normed, jnp.zeros((1, D), jnp.bfloat16)], axis=0)
    grouped = gate_up.reshape(EXPERTS, SLICES, D, 2 * HID_DEV)
    gate_cols = jnp.transpose(grouped[..., :HID_DEV], (0, 2, 1, 3)).reshape(EXPERTS, D, HID)
    up_cols = jnp.transpose(grouped[..., HID_DEV:], (0, 2, 1, 3)).reshape(EXPERTS, D, HID)
    down_rows = down_weight.reshape(EXPERTS, HID, D)
    zero_gate = jnp.zeros((1,), gates.dtype)

    def expert_step(total, index):
        hits = routes == index
        marked = jnp.any(hits, axis=1)
        weight = lax.optimization_barrier(jnp.sum(jnp.where(hits, gates, 0.0), axis=1))
        chosen = jnp.nonzero(marked, size=REQS * CAPACITY, fill_value=TOKENS)[0].astype(jnp.int32)
        rows = padded[chosen]
        gate = jnp.dot(rows, gate_cols[index], preferred_element_type=jnp.float32)
        upper = jnp.dot(rows, up_cols[index], preferred_element_type=jnp.float32)
        hidden = (jax.nn.silu(gate) * upper).astype(jnp.bfloat16)
        produced = jnp.dot(hidden, down_rows[index], preferred_element_type=jnp.float32).astype(jnp.bfloat16)
        scale = jnp.concatenate([weight, zero_gate], axis=0)[chosen]
        total = total.at[chosen].add(produced.astype(jnp.float32) * scale[:, None], mode='drop')
        return (total, None)
    start = jnp.zeros((TOKENS, D), jnp.float32)
    total, _ = lax.scan(expert_step, start, jnp.arange(EXPERTS, dtype=jnp.int32))
    return (branch.astype(jnp.bfloat16), total.astype(jnp.bfloat16))
```

```python
import jax
import jax.numpy as jnp
from jax import lax
from jax.sharding import PartitionSpec as P

HEADS = 16
KV_HEADS = 8
HEAD = 64
EXPERTS = 32
TOP = 8
CAPACITY = 40


def rms_scale(values, gain):
    wide = values.astype(jnp.float32)
    power = jnp.mean(wide * wide, axis=-1, keepdims=True)
    return wide * lax.rsqrt(power + 1e-06) * gain


def rotate(vectors, places):
    half = vectors.shape[-1] // 2
    freq = 10000.0 ** (-jnp.arange(half, dtype=jnp.float32) / half)
    angle = places[:, None] * freq[None, :]
    cosine = jnp.cos(angle)[:, None, :]
    sine = jnp.sin(angle)[:, None, :]
    first = vectors[..., :half]
    second = vectors[..., half:]
    return jnp.concatenate(
        [first * cosine - second * sine, second * cosine + first * sine], axis=-1
    )


def attend(tokens, qkv_weight, out_weight, norm_attn, keys_cache, values_cache, length):
    rows = tokens.shape[0]
    span = keys_cache.shape[0]
    qwidth = HEADS * HEAD
    kvwidth = KV_HEADS * HEAD
    normed = rms_scale(tokens, norm_attn).astype(jnp.bfloat16)
    mixed = jnp.dot(normed, qkv_weight, preferred_element_type=jnp.float32)
    places = (length + jnp.arange(rows, dtype=jnp.int32)).astype(jnp.float32)
    query = rotate(mixed[:, :qwidth].reshape(rows, HEADS, HEAD), places).astype(jnp.bfloat16)
    key_new = rotate(
        mixed[:, qwidth : qwidth + kvwidth].reshape(rows, KV_HEADS, HEAD), places
    ).astype(jnp.bfloat16)
    value_new = mixed[:, qwidth + kvwidth :].astype(jnp.bfloat16)
    keys = jnp.concatenate([keys_cache, key_new.reshape(rows, kvwidth)], axis=0).reshape(
        span + rows, KV_HEADS, HEAD
    )
    values = jnp.concatenate([values_cache, value_new], axis=0).reshape(span + rows, KV_HEADS, HEAD)
    query = query.reshape(rows, KV_HEADS, HEADS // KV_HEADS, HEAD)
    scores = (
        jnp.einsum("tkgd,skd->kgts", query, keys, preferred_element_type=jnp.float32) * 0.015625
    )
    column = jnp.arange(span + rows, dtype=jnp.int32)[None, :]
    row_index = jnp.arange(rows, dtype=jnp.int32)[:, None]
    valid = jnp.where(column < span, column < length, column - span <= row_index)
    scores = jnp.where(valid[None, None], scores, -1e30)
    top = jnp.max(scores, axis=-1, keepdims=True)
    weights = jnp.exp(scores - top)
    weights = (weights / jnp.sum(weights, axis=-1, keepdims=True)).astype(jnp.bfloat16)
    heads_out = jnp.einsum("kgts,skd->tkgd", weights, values, preferred_element_type=jnp.float32)
    heads_out = heads_out.astype(jnp.bfloat16).reshape(rows, qwidth)
    return jnp.dot(heads_out, out_weight, preferred_element_type=jnp.float32)


def gather_expert(piece, slices):
    cuts = lax.axis_size("cuts")
    pieces = [piece]
    for shift in range(1, slices):
        pairs = [(i, (i // slices) * slices + (i % slices + shift) % slices) for i in range(cuts)]
        pieces.append(lax.ppermute(piece, "cuts", pairs))
    return pieces


def on_device(
    tokens,
    qkv_weight,
    out_weight,
    norm_attn,
    norm_expert,
    keys_cache,
    values_cache,
    lengths,
    routes,
    gates,
    gate_up,
    down_weight,
):
    groups = lax.axis_size("req")
    slices = groups * lax.axis_size("cuts") // EXPERTS
    width_dev = down_weight.shape[1]
    gate_up_all = jnp.concatenate(gather_expert(gate_up[0], slices), axis=1)
    down_all = jnp.concatenate(gather_expert(down_weight[0], slices), axis=0)
    branch = attend(
        tokens, qkv_weight, out_weight, norm_attn, keys_cache[0], values_cache[0], lengths[0]
    )
    carried = tokens.astype(jnp.float32) + 0.22 * branch
    normed = rms_scale(carried, norm_expert).astype(jnp.bfloat16)
    rows = tokens.shape[0]
    width = tokens.shape[1]
    capacity = CAPACITY
    hits = routes[:, :, None] == jnp.arange(EXPERTS, dtype=jnp.int32)[None, None, :]
    marks = jnp.any(hits, axis=1)
    weight = jnp.sum(jnp.where(hits, gates[:, :, None], 0.0), axis=1)
    lower = (
        jnp.arange(rows, dtype=jnp.int32)[:, None] > jnp.arange(rows, dtype=jnp.int32)[None, :]
    ).astype(jnp.bfloat16)
    before = jnp.dot(lower, marks.astype(jnp.bfloat16), preferred_element_type=jnp.float32)
    slot = before.astype(jnp.int32)
    taken = marks[:, :, None] & (
        slot[:, :, None] == jnp.arange(capacity, dtype=jnp.int32)[None, None, :]
    )
    pick = taken.reshape(rows, EXPERTS * capacity)
    outgoing = jnp.dot(
        pick.astype(jnp.bfloat16).T, normed, preferred_element_type=jnp.float32
    ).astype(jnp.bfloat16)
    received = lax.all_to_all(
        outgoing.reshape(EXPERTS * slices, capacity // slices, width),
        ("req", "cuts"),
        split_axis=0,
        concat_axis=0,
        tiled=True,
    ).reshape(-1, width)
    both = jnp.dot(received, gate_up_all, preferred_element_type=jnp.float32)
    both = both.reshape(-1, slices, 2 * width_dev)
    hidden = (jax.nn.silu(both[..., :width_dev]) * both[..., width_dev:]).astype(jnp.bfloat16)
    produced = jnp.dot(
        hidden.reshape(-1, slices * width_dev), down_all, preferred_element_type=jnp.float32
    ).astype(jnp.bfloat16)
    results = lax.all_to_all(
        produced.reshape(EXPERTS * slices, capacity // slices, width),
        ("req", "cuts"),
        split_axis=0,
        concat_axis=0,
        tiled=True,
    ).reshape(EXPERTS * capacity, width)
    scale = jnp.where(pick, jnp.repeat(weight, capacity, axis=1), 0.0)
    mix = jnp.dot(
        scale,
        results.astype(jnp.float32),
        precision=lax.Precision.HIGHEST,
        preferred_element_type=jnp.float32,
    )
    return (branch.astype(jnp.bfloat16), mix.astype(jnp.bfloat16))


def solution(mesh):
    placed = (
        P(("req", "cuts"), None),
        P(),
        P(),
        P(),
        P(),
        P(("req", "cuts"), None, None),
        P(("req", "cuts"), None, None),
        P(("req", "cuts")),
        P(("req", "cuts"), None),
        P(("req", "cuts"), None),
        P(("req", "cuts"), None, None),
        P(("req", "cuts"), None, None),
    )
    return jax.shard_map(
        on_device,
        mesh=mesh,
        in_specs=placed,
        out_specs=(P(("req", "cuts"), None), P(("req", "cuts"), None)),
        check_vma=False,
    )
```

```python
import jax
import jax.numpy as jnp
from jax import lax
from jax.sharding import PartitionSpec as P

HEADS = 16
KV_HEADS = 8
HEAD = 64
EXPERTS = 32
TOP = 8
CAPACITY = 40


def rms_scale(values, gain):
    wide = values.astype(jnp.float32)
    power = jnp.mean(wide * wide, axis=-1, keepdims=True)
    return wide * lax.rsqrt(power + 1e-06) * gain


def rotate(vectors, places):
    half = vectors.shape[-1] // 2
    freq = 10000.0 ** (-jnp.arange(half, dtype=jnp.float32) / half)
    angle = places[:, None] * freq[None, :]
    cosine = jnp.cos(angle)[:, None, :]
    sine = jnp.sin(angle)[:, None, :]
    first = vectors[..., :half]
    second = vectors[..., half:]
    return jnp.concatenate(
        [first * cosine - second * sine, second * cosine + first * sine], axis=-1
    )


def attend(tokens, qkv_weight, out_weight, norm_attn, keys_cache, values_cache, length):
    rows = tokens.shape[0]
    span = keys_cache.shape[0]
    qwidth = HEADS * HEAD
    kvwidth = KV_HEADS * HEAD
    normed = rms_scale(tokens, norm_attn).astype(jnp.bfloat16)
    mixed = jnp.dot(normed, qkv_weight, preferred_element_type=jnp.float32)
    places = (length + jnp.arange(rows, dtype=jnp.int32)).astype(jnp.float32)
    query = rotate(mixed[:, :qwidth].reshape(rows, HEADS, HEAD), places).astype(jnp.bfloat16)
    key_new = rotate(
        mixed[:, qwidth : qwidth + kvwidth].reshape(rows, KV_HEADS, HEAD), places
    ).astype(jnp.bfloat16)
    value_new = mixed[:, qwidth + kvwidth :].astype(jnp.bfloat16)
    keys = jnp.concatenate([keys_cache, key_new.reshape(rows, kvwidth)], axis=0).reshape(
        span + rows, KV_HEADS, HEAD
    )
    values = jnp.concatenate([values_cache, value_new], axis=0).reshape(span + rows, KV_HEADS, HEAD)
    query = query.reshape(rows, KV_HEADS, HEADS // KV_HEADS, HEAD)
    scores = (
        jnp.einsum("tkgd,skd->kgts", query, keys, preferred_element_type=jnp.float32) * 0.015625
    )
    column = jnp.arange(span + rows, dtype=jnp.int32)[None, :]
    row_index = jnp.arange(rows, dtype=jnp.int32)[:, None]
    valid = jnp.where(column < span, column < length, column - span <= row_index)
    scores = jnp.where(valid[None, None], scores, -1e30)
    top = jnp.max(scores, axis=-1, keepdims=True)
    weights = jnp.exp(scores - top)
    weights = (weights / jnp.sum(weights, axis=-1, keepdims=True)).astype(jnp.bfloat16)
    heads_out = jnp.einsum("kgts,skd->tkgd", weights, values, preferred_element_type=jnp.float32)
    heads_out = heads_out.astype(jnp.bfloat16).reshape(rows, qwidth)
    return jnp.dot(heads_out, out_weight, preferred_element_type=jnp.float32)


def on_device(
    tokens,
    qkv_weight,
    out_weight,
    norm_attn,
    norm_expert,
    keys_cache,
    values_cache,
    lengths,
    routes,
    gates,
    gate_up,
    down_weight,
):
    slices = lax.axis_size("q")
    width_dev = down_weight.shape[1]
    gate_up_all = lax.all_gather(gate_up[0], "q", axis=1, tiled=True)
    down_all = lax.all_gather(down_weight[0], "q", axis=0, tiled=True)
    branch = attend(
        tokens, qkv_weight, out_weight, norm_attn, keys_cache[0], values_cache[0], lengths[0]
    )
    carried = tokens.astype(jnp.float32) + 0.22 * branch
    normed = rms_scale(carried, norm_expert).astype(jnp.bfloat16)
    rows = tokens.shape[0]
    capacity = CAPACITY
    hits = routes[:, :, None] == jnp.arange(EXPERTS, dtype=jnp.int32)[None, None, :]
    marks = jnp.any(hits, axis=1)
    weight = jnp.sum(jnp.where(hits, gates[:, :, None], 0.0), axis=1)
    lower = (
        jnp.arange(rows, dtype=jnp.int32)[:, None] > jnp.arange(rows, dtype=jnp.int32)[None, :]
    ).astype(jnp.bfloat16)
    before = jnp.dot(lower, marks.astype(jnp.bfloat16), preferred_element_type=jnp.float32)
    slot = before.astype(jnp.int32)
    pick = marks[:, :, None] & (
        slot[:, :, None] == jnp.arange(capacity, dtype=jnp.int32)[None, None, :]
    )
    outgoing = jnp.einsum(
        "tec,tw->ecw", pick.astype(jnp.bfloat16), normed, preferred_element_type=jnp.float32
    ).astype(jnp.bfloat16)
    received = lax.all_to_all(outgoing, ("req", "h"), split_axis=0, concat_axis=0, tiled=True)
    both = jnp.einsum("scw,wh->sch", received, gate_up_all, preferred_element_type=jnp.float32)
    both = both.reshape(both.shape[0], both.shape[1], slices, 2 * width_dev)
    hidden = (jax.nn.silu(both[..., :width_dev]) * both[..., width_dev:]).astype(jnp.bfloat16)
    hidden = hidden.reshape(both.shape[0], both.shape[1], slices * width_dev)
    produced = jnp.einsum(
        "sch,hw->scw", hidden, down_all, preferred_element_type=jnp.float32
    ).astype(jnp.bfloat16)
    results = lax.all_to_all(produced, ("req", "h"), split_axis=0, concat_axis=0, tiled=True)
    scale = jnp.where(pick, weight[:, :, None], 0.0)
    mix = jnp.einsum(
        "tec,ecw->tw",
        scale,
        results.astype(jnp.float32),
        precision=lax.Precision.HIGHEST,
        preferred_element_type=jnp.float32,
    )
    return (branch.astype(jnp.bfloat16), mix.astype(jnp.bfloat16))


def solution(mesh):
    groups = mesh.shape["req"]
    slices = groups * mesh.shape["cuts"] // EXPERTS
    split = jax.sharding.Mesh(
        mesh.devices.reshape(groups, mesh.shape["cuts"] // slices, slices), ("req", "h", "q")
    )
    rows = ("req", "h", "q")
    placed = (
        P(rows, None),
        P(),
        P(),
        P(),
        P(),
        P(rows, None, None),
        P(rows, None, None),
        P(rows),
        P(rows, None),
        P(rows, None),
        P(rows, None, None),
        P(rows, None, None),
    )
    return jax.shard_map(
        on_device,
        mesh=split,
        in_specs=placed,
        out_specs=(P(rows, None), P(rows, None)),
        check_vma=False,
    )
```

```python
import jax
import jax.numpy as jnp
from jax import lax
from jax.sharding import PartitionSpec as P
from jax.experimental import pallas as pl
from jax.experimental.pallas import tpu as pltpu

HEADS = 16
KV_HEADS = 8
HEAD = 64
EXPERTS = 32
TOP = 8
CAPACITY = 40


def rms_scale(values, gain):
    wide = values.astype(jnp.float32)
    power = jnp.mean(wide * wide, axis=-1, keepdims=True)
    return wide * lax.rsqrt(power + 1e-06) * gain


def rotate(vectors, places):
    half = vectors.shape[-1] // 2
    freq = 10000.0 ** (-jnp.arange(half, dtype=jnp.float32) / half)
    angle = places[:, None] * freq[None, :]
    cosine = jnp.cos(angle)[:, None, :]
    sine = jnp.sin(angle)[:, None, :]
    first = vectors[..., :half]
    second = vectors[..., half:]
    return jnp.concatenate(
        [first * cosine - second * sine, second * cosine + first * sine], axis=-1
    )


def attention_kernel(length_ref, q_ref, kc_ref, vc_ref, kn_ref, vn_ref, o_ref):
    length = length_ref[0]
    span = kc_ref.shape[0]
    rows = kn_ref.shape[0]
    kc = kc_ref[...]
    vc = vc_ref[...]
    kn = kn_ref[...]
    vn = vn_ref[...]
    column = lax.broadcasted_iota(jnp.int32, (rows, span), 1)
    cache_ok = column < length
    new_col = lax.broadcasted_iota(jnp.int32, (rows, rows), 1)
    new_row = lax.broadcasted_iota(jnp.int32, (rows, rows), 0)
    new_ok = new_col <= new_row
    contract = (((1,), (1,)), ((), ()))
    for j in range(q_ref.shape[0]):
        q = q_ref[j]
        s = lax.dot_general(q, kc, contract, preferred_element_type=jnp.float32) * 0.015625
        s = jnp.where(cache_ok, s, -1e30)
        sn = lax.dot_general(q, kn, contract, preferred_element_type=jnp.float32) * 0.015625
        sn = jnp.where(new_ok, sn, -1e30)
        top = jnp.maximum(jnp.max(s, axis=1, keepdims=True), jnp.max(sn, axis=1, keepdims=True))
        e = jnp.exp(s - top)
        en = jnp.exp(sn - top)
        total = jnp.sum(e, axis=1, keepdims=True) + jnp.sum(en, axis=1, keepdims=True)
        w = (e / total).astype(jnp.bfloat16)
        wn = (en / total).astype(jnp.bfloat16)
        o = jnp.dot(w, vc, preferred_element_type=jnp.float32) + jnp.dot(
            wn, vn, preferred_element_type=jnp.float32
        )
        o_ref[j] = o.astype(jnp.bfloat16)


def attention_core(length, q_pairs, kc, vc, kn, vn, interpret=False):
    heads, rows, lanes = q_pairs.shape
    span = kc.shape[0]
    pairs = kc.shape[1] // lanes
    per = heads // pairs
    return pl.pallas_call(
        attention_kernel,
        grid_spec=pltpu.PrefetchScalarGridSpec(
            num_scalar_prefetch=1,
            grid=(pairs,),
            in_specs=[
                pl.BlockSpec((per, rows, lanes), lambda p, n: (p, 0, 0)),
                pl.BlockSpec((span, lanes), lambda p, n: (0, p)),
                pl.BlockSpec((span, lanes), lambda p, n: (0, p)),
                pl.BlockSpec((rows, lanes), lambda p, n: (0, p)),
                pl.BlockSpec((rows, lanes), lambda p, n: (0, p)),
            ],
            out_specs=pl.BlockSpec((per, rows, lanes), lambda p, n: (p, 0, 0)),
        ),
        out_shape=jax.ShapeDtypeStruct((heads, rows, lanes), jnp.bfloat16),
        interpret=interpret,
    )(length, q_pairs, kc, vc, kn, vn)


def attend(tokens, qkv_weight, out_weight, norm_attn, keys_cache, values_cache, length, interpret=False):
    rows = tokens.shape[0]
    qwidth = HEADS * HEAD
    kvwidth = KV_HEADS * HEAD
    lanes = 2 * HEAD
    normed = rms_scale(tokens, norm_attn).astype(jnp.bfloat16)
    mixed = jnp.dot(normed, qkv_weight, preferred_element_type=jnp.float32)
    places = (length + jnp.arange(rows, dtype=jnp.int32)).astype(jnp.float32)
    query = rotate(mixed[:, :qwidth].reshape(rows, HEADS, HEAD), places).astype(jnp.bfloat16)
    key_new = rotate(
        mixed[:, qwidth : qwidth + kvwidth].reshape(rows, KV_HEADS, HEAD), places
    ).astype(jnp.bfloat16)
    value_new = mixed[:, qwidth + kvwidth :].astype(jnp.bfloat16)
    group = HEADS // KV_HEADS
    half = (jnp.arange(HEADS) // group) % 2
    lane_half = jnp.arange(lanes) // HEAD
    doubled = jnp.concatenate([query, query], axis=-1)
    q_pairs = jnp.where((lane_half[None, :] == half[:, None])[None], doubled, 0)
    q_pairs = jnp.transpose(q_pairs, (1, 0, 2)).astype(jnp.bfloat16)
    paired = attention_core(
        length.reshape(1).astype(jnp.int32),
        q_pairs,
        keys_cache,
        values_cache,
        key_new.reshape(rows, kvwidth),
        value_new,
        interpret=interpret,
    )
    split = paired.reshape(HEADS, rows, 2, HEAD)
    chosen = jnp.where((half == 0)[:, None, None], split[:, :, 0, :], split[:, :, 1, :])
    heads_out = jnp.transpose(chosen, (1, 0, 2)).reshape(rows, qwidth)
    return jnp.dot(heads_out, out_weight, preferred_element_type=jnp.float32)


def on_device(
    tokens,
    qkv_weight,
    out_weight,
    norm_attn,
    norm_expert,
    keys_cache,
    values_cache,
    lengths,
    routes,
    gates,
    gate_up,
    down_weight,
):
    slices = lax.axis_size("q")
    width_dev = down_weight.shape[1]
    gate_up_all = lax.all_gather(gate_up[0], "q", axis=1, tiled=True)
    down_all = lax.all_gather(down_weight[0], "q", axis=0, tiled=True)
    branch = attend(
        tokens, qkv_weight, out_weight, norm_attn, keys_cache[0], values_cache[0], lengths[0]
    )
    branch, gate_up_all, down_all = lax.optimization_barrier((branch, gate_up_all, down_all))
    carried = tokens.astype(jnp.float32) + 0.22 * branch
    normed = rms_scale(carried, norm_expert).astype(jnp.bfloat16)
    rows = tokens.shape[0]
    capacity = CAPACITY
    hits = routes[:, :, None] == jnp.arange(EXPERTS, dtype=jnp.int32)[None, None, :]
    marks = jnp.any(hits, axis=1)
    weight = jnp.sum(jnp.where(hits, gates[:, :, None], 0.0), axis=1)
    lower = (
        jnp.arange(rows, dtype=jnp.int32)[:, None] > jnp.arange(rows, dtype=jnp.int32)[None, :]
    ).astype(jnp.bfloat16)
    before = jnp.dot(lower, marks.astype(jnp.bfloat16), preferred_element_type=jnp.float32)
    slot = before.astype(jnp.int32)
    pick = marks[:, :, None] & (
        slot[:, :, None] == jnp.arange(capacity, dtype=jnp.int32)[None, None, :]
    )
    outgoing = jnp.einsum(
        "tec,tw->ecw", pick.astype(jnp.bfloat16), normed, preferred_element_type=jnp.float32
    ).astype(jnp.bfloat16)
    received = lax.all_to_all(outgoing, ("req", "h"), split_axis=0, concat_axis=0, tiled=True)
    pieces = gate_up_all.reshape(gate_up_all.shape[0], slices, 2 * width_dev)
    gate_cols = pieces[..., :width_dev].reshape(gate_up_all.shape[0], slices * width_dev)
    up_cols = pieces[..., width_dev:].reshape(gate_up_all.shape[0], slices * width_dev)
    gate = jnp.einsum("scw,wh->sch", received, gate_cols, preferred_element_type=jnp.float32)
    upper = jnp.einsum("scw,wh->sch", received, up_cols, preferred_element_type=jnp.float32)
    hidden = (jax.nn.silu(gate) * upper).astype(jnp.bfloat16)
    produced = jnp.einsum(
        "sch,hw->scw", hidden, down_all, preferred_element_type=jnp.float32
    ).astype(jnp.bfloat16)
    results = lax.all_to_all(produced, ("req", "h"), split_axis=0, concat_axis=0, tiled=True)
    scale = jnp.where(pick, weight[:, :, None], 0.0)
    mix = jnp.einsum(
        "tec,ecw->tw",
        scale,
        results.astype(jnp.float32),
        precision=lax.Precision.HIGHEST,
        preferred_element_type=jnp.float32,
    )
    return (branch.astype(jnp.bfloat16), mix.astype(jnp.bfloat16))


def solution(mesh):
    groups = mesh.shape["req"]
    slices = groups * mesh.shape["cuts"] // EXPERTS
    split = jax.sharding.Mesh(
        mesh.devices.reshape(groups, mesh.shape["cuts"] // slices, slices), ("req", "h", "q")
    )
    rows = ("req", "h", "q")
    placed = (
        P(rows, None),
        P(),
        P(),
        P(),
        P(),
        P(rows, None, None),
        P(rows, None, None),
        P(rows),
        P(rows, None),
        P(rows, None),
        P(rows, None, None),
        P(rows, None, None),
    )
    return jax.shard_map(
        on_device,
        mesh=split,
        in_specs=placed,
        out_specs=(P(rows, None), P(rows, None)),
        check_vma=False,
    )
```

```python
import jax
import jax.numpy as jnp
from jax import lax
from jax.sharding import PartitionSpec as P
from jax.experimental import pallas as pl
from jax.experimental.pallas import tpu as pltpu

HEADS = 16
KV_HEADS = 8
HEAD = 64
EXPERTS = 32
TOP = 8
CAPACITY = 40


def rms_scale(values, gain):
    wide = values.astype(jnp.float32)
    power = jnp.mean(wide * wide, axis=-1, keepdims=True)
    return wide * lax.rsqrt(power + 1e-06) * gain


def rotate(vectors, places):
    half = vectors.shape[-1] // 2
    freq = 10000.0 ** (-jnp.arange(half, dtype=jnp.float32) / half)
    angle = places[:, None] * freq[None, :]
    cosine = jnp.cos(angle)[:, None, :]
    sine = jnp.sin(angle)[:, None, :]
    first = vectors[..., :half]
    second = vectors[..., half:]
    return jnp.concatenate(
        [first * cosine - second * sine, second * cosine + first * sine], axis=-1
    )


def attention_kernel(length_ref, q_ref, kc_ref, vc_ref, kn_ref, vn_ref, o_ref):
    length = length_ref[0]
    span, lanes = kc_ref.shape
    rows = kn_ref.shape[0]
    half = lanes // 2
    kc = kc_ref[...]
    vc = vc_ref[...]
    kn = kn_ref[...]
    vn = vn_ref[...]
    column = lax.broadcasted_iota(jnp.int32, (rows, span), 1)
    cache_ok = column < length
    new_col = lax.broadcasted_iota(jnp.int32, (rows, rows), 1)
    new_row = lax.broadcasted_iota(jnp.int32, (rows, rows), 0)
    new_ok = new_col <= new_row
    low = lax.broadcasted_iota(jnp.int32, (rows, lanes), 1) < half
    first = q_ref[:, :lanes].astype(jnp.float32)
    second = q_ref[:, lanes:].astype(jnp.float32)
    queries = (
        jnp.where(low, first, 0.0),
        jnp.where(low, pltpu.roll(first, half, 1), 0.0),
        jnp.where(low, 0.0, pltpu.roll(second, half, 1)),
        jnp.where(low, 0.0, second),
    )
    contract = (((1,), (1,)), ((), ()))
    outs = []
    for q in queries:
        q = q.astype(jnp.bfloat16)
        s = lax.dot_general(q, kc, contract, preferred_element_type=jnp.float32)
        s = jnp.where(cache_ok, s, -1e30)
        sn = lax.dot_general(q, kn, contract, preferred_element_type=jnp.float32)
        sn = jnp.where(new_ok, sn, -1e30)
        top = jnp.maximum(jnp.max(s, axis=1, keepdims=True), jnp.max(sn, axis=1, keepdims=True))
        e = jnp.exp(s - top)
        en = jnp.exp(sn - top)
        total = jnp.sum(e, axis=1, keepdims=True) + jnp.sum(en, axis=1, keepdims=True)
        inverse = 1.0 / total
        w = (e * inverse).astype(jnp.bfloat16)
        wn = (en * inverse).astype(jnp.bfloat16)
        o = jnp.dot(w, vc, preferred_element_type=jnp.float32) + jnp.dot(
            wn, vn, preferred_element_type=jnp.float32
        )
        outs.append(o.astype(jnp.bfloat16).astype(jnp.float32))
    left = jnp.where(low, outs[0], pltpu.roll(outs[1], half, 1))
    right = jnp.where(low, pltpu.roll(outs[2], half, 1), outs[3])
    o_ref[:, :lanes] = left.astype(jnp.bfloat16)
    o_ref[:, lanes:] = right.astype(jnp.bfloat16)


def attention_core(length, query, kc, vc, kn, vn, interpret=False):
    rows, qwidth = query.shape
    span, kvwidth = kc.shape
    lanes = 2 * HEAD
    pairs = kvwidth // lanes
    qblock = qwidth // pairs
    return pl.pallas_call(
        attention_kernel,
        grid_spec=pltpu.PrefetchScalarGridSpec(
            num_scalar_prefetch=1,
            grid=(pairs,),
            in_specs=[
                pl.BlockSpec((rows, qblock), lambda p, n: (0, p)),
                pl.BlockSpec((span, lanes), lambda p, n: (0, p)),
                pl.BlockSpec((span, lanes), lambda p, n: (0, p)),
                pl.BlockSpec((rows, lanes), lambda p, n: (0, p)),
                pl.BlockSpec((rows, lanes), lambda p, n: (0, p)),
            ],
            out_specs=pl.BlockSpec((rows, qblock), lambda p, n: (0, p)),
        ),
        out_shape=jax.ShapeDtypeStruct((rows, qwidth), jnp.bfloat16),
        interpret=interpret,
    )(length, query, kc, vc, kn, vn)


def rotate_lanes(values, places):
    half = HEAD // 2
    freq = 10000.0 ** (-jnp.arange(half, dtype=jnp.float32) / half)
    angle = places[:, None] * freq[None, :]
    repeat = values.shape[1] // half
    cosine = jnp.tile(jnp.cos(angle), (1, repeat))
    sine = jnp.tile(jnp.sin(angle), (1, repeat))
    lead = (jnp.arange(values.shape[1]) % HEAD < half)[None, :]
    partner = jnp.where(lead, jnp.roll(values, -half, axis=1), jnp.roll(values, half, axis=1))
    return jnp.where(lead, values * cosine - partner * sine, values * cosine + partner * sine)


def attend(tokens, qkv_weight, out_weight, norm_attn, keys_cache, values_cache, length, interpret=False):
    rows = tokens.shape[0]
    qwidth = HEADS * HEAD
    kvwidth = KV_HEADS * HEAD
    normed = rms_scale(tokens, norm_attn).astype(jnp.bfloat16)
    mixed = jnp.dot(normed, qkv_weight, preferred_element_type=jnp.float32)
    places = (length + jnp.arange(rows, dtype=jnp.int32)).astype(jnp.float32)
    turned = rotate_lanes(mixed[:, : qwidth + kvwidth], places)
    query = (turned[:, :qwidth].astype(jnp.bfloat16) * 0.015625).astype(jnp.bfloat16)
    key_new = turned[:, qwidth:].astype(jnp.bfloat16)
    value_new = mixed[:, qwidth + kvwidth :].astype(jnp.bfloat16)
    heads_out = attention_core(
        length.reshape(1).astype(jnp.int32),
        query,
        keys_cache,
        values_cache,
        key_new,
        value_new,
        interpret=interpret,
    )
    return jnp.dot(heads_out, out_weight, preferred_element_type=jnp.float32)


def gather_expert(piece):
    near = lax.ppermute(piece, "q", [(i, i ^ 2) for i in range(4)])
    return [
        piece,
        near,
        lax.ppermute(piece, "q", [(i, i ^ 1) for i in range(4)]),
        lax.ppermute(near, "q", [(i, i ^ 1) for i in range(4)]),
    ]


def on_device(
    tokens,
    qkv_weight,
    out_weight,
    norm_attn,
    norm_expert,
    keys_cache,
    values_cache,
    lengths,
    routes,
    gates,
    gate_up,
    down_weight,
):
    slices = lax.axis_size("q")
    width_dev = down_weight.shape[1]
    gate_up_all = jnp.concatenate(gather_expert(gate_up[0]), axis=1)
    down_all = jnp.concatenate(gather_expert(down_weight[0]), axis=0)
    branch = attend(
        tokens, qkv_weight, out_weight, norm_attn, keys_cache[0], values_cache[0], lengths[0]
    )
    branch, gate_up_all, down_all = lax.optimization_barrier((branch, gate_up_all, down_all))
    carried = tokens.astype(jnp.float32) + 0.22 * branch
    normed = rms_scale(carried, norm_expert).astype(jnp.bfloat16)
    rows = tokens.shape[0]
    capacity = CAPACITY
    hits = routes[:, :, None] == jnp.arange(EXPERTS, dtype=jnp.int32)[None, None, :]
    marks = jnp.any(hits, axis=1)
    weight = jnp.sum(jnp.where(hits, gates[:, :, None], 0.0), axis=1)
    lower = (
        jnp.arange(rows, dtype=jnp.int32)[:, None] > jnp.arange(rows, dtype=jnp.int32)[None, :]
    ).astype(jnp.bfloat16)
    before = jnp.dot(lower, marks.astype(jnp.bfloat16), preferred_element_type=jnp.float32)
    slot = before.astype(jnp.int32)
    pick = marks[:, :, None] & (
        slot[:, :, None] == jnp.arange(capacity, dtype=jnp.int32)[None, None, :]
    )
    outgoing = jnp.einsum(
        "tec,tw->ecw", pick.astype(jnp.bfloat16), normed, preferred_element_type=jnp.float32
    ).astype(jnp.bfloat16)
    received = lax.all_to_all(outgoing, ("req", "h"), split_axis=0, concat_axis=0, tiled=True)
    pieces = gate_up_all.reshape(gate_up_all.shape[0], slices, 2 * width_dev)
    gate_cols = pieces[..., :width_dev].reshape(gate_up_all.shape[0], slices * width_dev)
    up_cols = pieces[..., width_dev:].reshape(gate_up_all.shape[0], slices * width_dev)
    gate = jnp.einsum("scw,wh->sch", received, gate_cols, preferred_element_type=jnp.float32)
    upper = jnp.einsum("scw,wh->sch", received, up_cols, preferred_element_type=jnp.float32)
    hidden = (jax.nn.silu(gate) * upper).astype(jnp.bfloat16)
    produced = jnp.einsum(
        "sch,hw->scw", hidden, down_all, preferred_element_type=jnp.float32
    ).astype(jnp.bfloat16)
    results = lax.all_to_all(produced, ("req", "h"), split_axis=0, concat_axis=0, tiled=True)
    scale = jnp.where(pick, weight[:, :, None], 0.0)
    mix = jnp.einsum(
        "tec,ecw->tw",
        scale,
        results.astype(jnp.float32),
        precision=lax.Precision.HIGHEST,
        preferred_element_type=jnp.float32,
    )
    return (branch.astype(jnp.bfloat16), mix.astype(jnp.bfloat16))


def solution(mesh):
    groups = mesh.shape["req"]
    slices = groups * mesh.shape["cuts"] // EXPERTS
    split = jax.sharding.Mesh(
        mesh.devices.reshape(groups, mesh.shape["cuts"] // slices, slices), ("req", "h", "q")
    )
    rows = ("req", "h", "q")
    placed = (
        P(rows, None),
        P(),
        P(),
        P(),
        P(),
        P(rows, None, None),
        P(rows, None, None),
        P(rows),
        P(rows, None),
        P(rows, None),
        P(rows, None, None),
        P(rows, None, None),
    )
    return jax.shard_map(
        on_device,
        mesh=split,
        in_specs=placed,
        out_specs=(P(rows, None), P(rows, None)),
        check_vma=False,
    )
```

```python
import jax
import jax.numpy as jnp
from jax import lax
from jax.sharding import PartitionSpec as P
from jax.experimental import pallas as pl
from jax.experimental.pallas import tpu as pltpu

HEADS = 16
KV_HEADS = 8
HEAD = 64
EXPERTS = 32
TOP = 8
CAPACITY = 40


def rms_scale(values, gain):
    wide = values.astype(jnp.float32)
    power = jnp.mean(wide * wide, axis=-1, keepdims=True)
    return wide * lax.rsqrt(power + 1e-06) * gain


def rotate(vectors, places):
    half = vectors.shape[-1] // 2
    freq = 10000.0 ** (-jnp.arange(half, dtype=jnp.float32) / half)
    angle = places[:, None] * freq[None, :]
    cosine = jnp.cos(angle)[:, None, :]
    sine = jnp.sin(angle)[:, None, :]
    first = vectors[..., :half]
    second = vectors[..., half:]
    return jnp.concatenate(
        [first * cosine - second * sine, second * cosine + first * sine], axis=-1
    )


def turn(values, cosine, sine, lead, half):
    partner = jnp.where(
        lead, pltpu.roll(values, values.shape[1] - half, 1), pltpu.roll(values, half, 1)
    )
    return jnp.where(lead, values * cosine - partner * sine, values * cosine + partner * sine)


def attention_kernel(length_ref, q_ref, k_ref, v_ref, cos_ref, sin_ref, kc_ref, vc_ref, o_ref):
    length = length_ref[0]
    span, lanes = kc_ref.shape
    rows = k_ref.shape[0]
    half = lanes // 2
    quarter = HEAD // 2
    cosine = cos_ref[...]
    sine = sin_ref[...]
    lane = lax.broadcasted_iota(jnp.int32, (rows, lanes), 1)
    lead = lane % HEAD < quarter
    low = lane < half
    kc = kc_ref[...]
    vc = vc_ref[...]
    kn = turn(k_ref[...], cosine, sine, lead, quarter).astype(jnp.bfloat16)
    vn = v_ref[...].astype(jnp.bfloat16)
    column = lax.broadcasted_iota(jnp.int32, (rows, span), 1)
    cache_ok = column < length
    new_col = lax.broadcasted_iota(jnp.int32, (rows, rows), 1)
    new_row = lax.broadcasted_iota(jnp.int32, (rows, rows), 0)
    new_ok = new_col <= new_row

    def scaled(values):
        rotated = turn(values, cosine, sine, lead, quarter).astype(jnp.bfloat16)
        return (rotated * 0.015625).astype(jnp.bfloat16).astype(jnp.float32)

    first = scaled(q_ref[:, :lanes])
    second = scaled(q_ref[:, lanes:])
    queries = (
        jnp.where(low, first, 0.0),
        jnp.where(low, pltpu.roll(first, half, 1), 0.0),
        jnp.where(low, 0.0, pltpu.roll(second, half, 1)),
        jnp.where(low, 0.0, second),
    )
    contract = (((1,), (1,)), ((), ()))
    outs = []
    for q in queries:
        q = q.astype(jnp.bfloat16)
        s = lax.dot_general(q, kc, contract, preferred_element_type=jnp.float32)
        s = jnp.where(cache_ok, s, -1e30)
        sn = lax.dot_general(q, kn, contract, preferred_element_type=jnp.float32)
        sn = jnp.where(new_ok, sn, -1e30)
        top = jnp.maximum(jnp.max(s, axis=1, keepdims=True), jnp.max(sn, axis=1, keepdims=True))
        e = jnp.exp(s - top)
        en = jnp.exp(sn - top)
        total = jnp.sum(e, axis=1, keepdims=True) + jnp.sum(en, axis=1, keepdims=True)
        inverse = 1.0 / total
        w = (e * inverse).astype(jnp.bfloat16)
        wn = (en * inverse).astype(jnp.bfloat16)
        o = jnp.dot(w, vc, preferred_element_type=jnp.float32) + jnp.dot(
            wn, vn, preferred_element_type=jnp.float32
        )
        outs.append(o.astype(jnp.bfloat16).astype(jnp.float32))
    left = jnp.where(low, outs[0], pltpu.roll(outs[1], half, 1))
    right = jnp.where(low, pltpu.roll(outs[2], half, 1), outs[3])
    o_ref[:, :lanes] = left.astype(jnp.bfloat16)
    o_ref[:, lanes:] = right.astype(jnp.bfloat16)


def attention_core(length, mixed, cosine, sine, kc, vc, interpret=False):
    rows = mixed.shape[0]
    span, kvwidth = kc.shape
    qwidth = HEADS * HEAD
    lanes = 2 * HEAD
    pairs = kvwidth // lanes
    qblock = qwidth // pairs
    kstart = qwidth // lanes
    vstart = kstart + pairs
    return pl.pallas_call(
        attention_kernel,
        grid_spec=pltpu.PrefetchScalarGridSpec(
            num_scalar_prefetch=1,
            grid=(pairs,),
            in_specs=[
                pl.BlockSpec((rows, qblock), lambda p, n: (0, p)),
                pl.BlockSpec((rows, lanes), lambda p, n: (0, kstart + p)),
                pl.BlockSpec((rows, lanes), lambda p, n: (0, vstart + p)),
                pl.BlockSpec((rows, lanes), lambda p, n: (0, 0)),
                pl.BlockSpec((rows, lanes), lambda p, n: (0, 0)),
                pl.BlockSpec((span, lanes), lambda p, n: (0, p)),
                pl.BlockSpec((span, lanes), lambda p, n: (0, p)),
            ],
            out_specs=pl.BlockSpec((rows, qblock), lambda p, n: (0, p)),
        ),
        out_shape=jax.ShapeDtypeStruct((rows, qwidth), jnp.bfloat16),
        interpret=interpret,
    )(length, mixed, mixed, mixed, cosine, sine, kc, vc)


def attend(tokens, qkv_weight, out_weight, norm_attn, keys_cache, values_cache, length, interpret=False):
    rows = tokens.shape[0]
    half = HEAD // 2
    normed = rms_scale(tokens, norm_attn).astype(jnp.bfloat16)
    mixed = jnp.dot(normed, qkv_weight, preferred_element_type=jnp.float32)
    places = (length + jnp.arange(rows, dtype=jnp.int32)).astype(jnp.float32)
    freq = 10000.0 ** (-jnp.arange(half, dtype=jnp.float32) / half)
    angle = places[:, None] * freq[None, :]
    cosine = jnp.tile(jnp.cos(angle), (1, 4))
    sine = jnp.tile(jnp.sin(angle), (1, 4))
    heads_out = attention_core(
        length.reshape(1).astype(jnp.int32),
        mixed,
        cosine,
        sine,
        keys_cache,
        values_cache,
        interpret=interpret,
    )
    return jnp.dot(heads_out, out_weight, preferred_element_type=jnp.float32)


def gather_expert(piece):
    near = lax.ppermute(piece, "q", [(i, i ^ 2) for i in range(4)])
    return [
        piece,
        near,
        lax.ppermute(piece, "q", [(i, i ^ 1) for i in range(4)]),
        lax.ppermute(near, "q", [(i, i ^ 1) for i in range(4)]),
    ]


def on_device(
    tokens,
    qkv_weight,
    out_weight,
    norm_attn,
    norm_expert,
    keys_cache,
    values_cache,
    lengths,
    routes,
    gates,
    gate_up,
    down_weight,
):
    slices = lax.axis_size("q")
    width_dev = down_weight.shape[1]
    gate_up_parts = gather_expert(gate_up[0])
    down_parts = gather_expert(down_weight[0])
    branch = attend(
        tokens, qkv_weight, out_weight, norm_attn, keys_cache[0], values_cache[0], lengths[0]
    )
    branch, gate_up_parts, down_parts = lax.optimization_barrier(
        (branch, gate_up_parts, down_parts)
    )
    gate_up_all = jnp.concatenate(gate_up_parts, axis=1)
    down_all = jnp.concatenate(down_parts, axis=0)
    carried = tokens.astype(jnp.float32) + 0.22 * branch
    normed = rms_scale(carried, norm_expert).astype(jnp.bfloat16)
    rows = tokens.shape[0]
    capacity = CAPACITY
    hits = routes[:, :, None] == jnp.arange(EXPERTS, dtype=jnp.int32)[None, None, :]
    marks = jnp.any(hits, axis=1)
    weight = jnp.sum(jnp.where(hits, gates[:, :, None], 0.0), axis=1)
    lower = (
        jnp.arange(rows, dtype=jnp.int32)[:, None] > jnp.arange(rows, dtype=jnp.int32)[None, :]
    ).astype(jnp.bfloat16)
    before = jnp.dot(lower, marks.astype(jnp.bfloat16), preferred_element_type=jnp.float32)
    slot = before.astype(jnp.int32)
    pick = marks[:, :, None] & (
        slot[:, :, None] == jnp.arange(capacity, dtype=jnp.int32)[None, None, :]
    )
    outgoing = jnp.einsum(
        "tec,tw->ecw", pick.astype(jnp.bfloat16), normed, preferred_element_type=jnp.float32
    ).astype(jnp.bfloat16)
    received = lax.all_to_all(outgoing, ("req", "h"), split_axis=0, concat_axis=0, tiled=True)
    pieces = gate_up_all.reshape(gate_up_all.shape[0], slices, 2 * width_dev)
    gate_cols = pieces[..., :width_dev].reshape(gate_up_all.shape[0], slices * width_dev)
    up_cols = pieces[..., width_dev:].reshape(gate_up_all.shape[0], slices * width_dev)
    gate = jnp.einsum("scw,wh->sch", received, gate_cols, preferred_element_type=jnp.float32)
    upper = jnp.einsum("scw,wh->sch", received, up_cols, preferred_element_type=jnp.float32)
    hidden = (jax.nn.silu(gate) * upper).astype(jnp.bfloat16)
    produced = jnp.einsum(
        "sch,hw->scw", hidden, down_all, preferred_element_type=jnp.float32
    ).astype(jnp.bfloat16)
    results = lax.all_to_all(produced, ("req", "h"), split_axis=0, concat_axis=0, tiled=True)
    scale = jnp.where(pick, weight[:, :, None], 0.0)
    mix = jnp.einsum(
        "tec,ecw->tw",
        scale,
        results.astype(jnp.float32),
        precision=lax.Precision.HIGHEST,
        preferred_element_type=jnp.float32,
    )
    return (branch.astype(jnp.bfloat16), mix.astype(jnp.bfloat16))


def solution(mesh):
    groups = mesh.shape["req"]
    slices = groups * mesh.shape["cuts"] // EXPERTS
    split = jax.sharding.Mesh(
        mesh.devices.reshape(groups, mesh.shape["cuts"] // slices, slices), ("req", "h", "q")
    )
    rows = ("req", "h", "q")
    placed = (
        P(rows, None),
        P(),
        P(),
        P(),
        P(),
        P(rows, None, None),
        P(rows, None, None),
        P(rows),
        P(rows, None),
        P(rows, None),
        P(rows, None, None),
        P(rows, None, None),
    )
    return jax.shard_map(
        on_device,
        mesh=split,
        in_specs=placed,
        out_specs=(P(rows, None), P(rows, None)),
        check_vma=False,
    )
```

```python
import jax
import jax.numpy as jnp
from jax import lax
from jax.sharding import PartitionSpec as P
from jax.experimental import pallas as pl
from jax.experimental.pallas import tpu as pltpu

HEADS = 16
KV_HEADS = 8
HEAD = 64
EXPERTS = 32
TOP = 8
CAPACITY = 40


def rms_scale(values, gain):
    wide = values.astype(jnp.float32)
    power = jnp.mean(wide * wide, axis=-1, keepdims=True)
    return wide * lax.rsqrt(power + 1e-06) * gain


def rotate(vectors, places):
    half = vectors.shape[-1] // 2
    freq = 10000.0 ** (-jnp.arange(half, dtype=jnp.float32) / half)
    angle = places[:, None] * freq[None, :]
    cosine = jnp.cos(angle)[:, None, :]
    sine = jnp.sin(angle)[:, None, :]
    first = vectors[..., :half]
    second = vectors[..., half:]
    return jnp.concatenate(
        [first * cosine - second * sine, second * cosine + first * sine], axis=-1
    )


def turn(values, cosine, sine, lead, half):
    partner = jnp.where(
        lead, pltpu.roll(values, values.shape[1] - half, 1), pltpu.roll(values, half, 1)
    )
    return jnp.where(lead, values * cosine - partner * sine, values * cosine + partner * sine)


def attention_kernel(length_ref, q_ref, k_ref, v_ref, cos_ref, sin_ref, kc_ref, vc_ref, o_ref):
    length = length_ref[0]
    span, lanes = kc_ref.shape
    rows = k_ref.shape[0]
    half = lanes // 2
    quarter = HEAD // 2
    cosine = cos_ref[...]
    sine = sin_ref[...]
    lane = lax.broadcasted_iota(jnp.int32, (rows, lanes), 1)
    lead = lane % HEAD < quarter
    low = lane < half
    kc = kc_ref[...]
    vc = vc_ref[...]
    kn = turn(k_ref[...], cosine, sine, lead, quarter).astype(jnp.bfloat16)
    vn = v_ref[...].astype(jnp.bfloat16)
    column = lax.broadcasted_iota(jnp.int32, (rows, span), 1)
    cache_ok = column < length
    new_col = lax.broadcasted_iota(jnp.int32, (rows, rows), 1)
    new_row = lax.broadcasted_iota(jnp.int32, (rows, rows), 0)
    new_ok = new_col <= new_row

    def scaled(values):
        rotated = turn(values, cosine, sine, lead, quarter).astype(jnp.bfloat16)
        return (rotated * 0.015625).astype(jnp.bfloat16).astype(jnp.float32)

    first = scaled(q_ref[:, :lanes])
    second = scaled(q_ref[:, lanes:])
    queries = (
        jnp.where(low, first, 0.0),
        jnp.where(low, pltpu.roll(first, half, 1), 0.0),
        jnp.where(low, 0.0, pltpu.roll(second, half, 1)),
        jnp.where(low, 0.0, second),
    )
    contract = (((1,), (1,)), ((), ()))
    outs = []
    for q in queries:
        q = q.astype(jnp.bfloat16)
        s = lax.dot_general(q, kc, contract, preferred_element_type=jnp.float32)
        s = jnp.where(cache_ok, s, -1e30)
        sn = lax.dot_general(q, kn, contract, preferred_element_type=jnp.float32)
        sn = jnp.where(new_ok, sn, -1e30)
        top = jnp.maximum(jnp.max(s, axis=1, keepdims=True), jnp.max(sn, axis=1, keepdims=True))
        e = jnp.exp(s - top)
        en = jnp.exp(sn - top)
        total = jnp.sum(e, axis=1, keepdims=True) + jnp.sum(en, axis=1, keepdims=True)
        inverse = 1.0 / total
        w = (e * inverse).astype(jnp.bfloat16)
        wn = (en * inverse).astype(jnp.bfloat16)
        o = jnp.dot(w, vc, preferred_element_type=jnp.float32) + jnp.dot(
            wn, vn, preferred_element_type=jnp.float32
        )
        outs.append(o.astype(jnp.bfloat16).astype(jnp.float32))
    left = jnp.where(low, outs[0], pltpu.roll(outs[1], half, 1))
    right = jnp.where(low, pltpu.roll(outs[2], half, 1), outs[3])
    o_ref[:, :lanes] = left.astype(jnp.bfloat16)
    o_ref[:, lanes:] = right.astype(jnp.bfloat16)


def attention_core(length, mixed, cosine, sine, kc, vc, interpret=False):
    rows = mixed.shape[0]
    span, kvwidth = kc.shape
    qwidth = HEADS * HEAD
    lanes = 2 * HEAD
    pairs = kvwidth // lanes
    qblock = qwidth // pairs
    kstart = qwidth // lanes
    vstart = kstart + pairs
    return pl.pallas_call(
        attention_kernel,
        grid_spec=pltpu.PrefetchScalarGridSpec(
            num_scalar_prefetch=1,
            grid=(pairs,),
            in_specs=[
                pl.BlockSpec((rows, qblock), lambda p, n: (0, p)),
                pl.BlockSpec((rows, lanes), lambda p, n: (0, kstart + p)),
                pl.BlockSpec((rows, lanes), lambda p, n: (0, vstart + p)),
                pl.BlockSpec((rows, lanes), lambda p, n: (0, 0)),
                pl.BlockSpec((rows, lanes), lambda p, n: (0, 0)),
                pl.BlockSpec((span, lanes), lambda p, n: (0, p)),
                pl.BlockSpec((span, lanes), lambda p, n: (0, p)),
            ],
            out_specs=pl.BlockSpec((rows, qblock), lambda p, n: (0, p)),
        ),
        out_shape=jax.ShapeDtypeStruct((rows, qwidth), jnp.bfloat16),
        interpret=interpret,
    )(length, mixed, mixed, mixed, cosine, sine, kc, vc)


def attend(tokens, qkv_weight, out_weight, norm_attn, keys_cache, values_cache, length, interpret=False):
    rows = tokens.shape[0]
    half = HEAD // 2
    normed = rms_scale(tokens, norm_attn).astype(jnp.bfloat16)
    mixed = jnp.dot(normed, qkv_weight, preferred_element_type=jnp.float32)
    places = (length + jnp.arange(rows, dtype=jnp.int32)).astype(jnp.float32)
    freq = 10000.0 ** (-jnp.arange(half, dtype=jnp.float32) / half)
    angle = places[:, None] * freq[None, :]
    cosine = jnp.tile(jnp.cos(angle), (1, 4))
    sine = jnp.tile(jnp.sin(angle), (1, 4))
    heads_out = attention_core(
        length.reshape(1).astype(jnp.int32),
        mixed,
        cosine,
        sine,
        keys_cache,
        values_cache,
        interpret=interpret,
    )
    return jnp.dot(heads_out, out_weight, preferred_element_type=jnp.float32)


def swap(piece, bit):
    return lax.ppermute(piece, "q", [(i, i ^ bit) for i in range(lax.axis_size("q"))])


def on_device(
    tokens,
    qkv_weight,
    out_weight,
    norm_attn,
    norm_expert,
    keys_cache,
    values_cache,
    lengths,
    routes,
    gates,
    gate_up,
    down_weight,
):
    slices = lax.axis_size("q")
    width_dev = down_weight.shape[1]
    own_gu = gate_up[0]
    own_dw = down_weight[0]
    far_gu = swap(own_gu, 2)
    far_dw = swap(own_dw, 2)
    side_gu = swap(own_gu, 1)
    side_dw = swap(own_dw, 1)
    branch = attend(
        tokens, qkv_weight, out_weight, norm_attn, keys_cache[0], values_cache[0], lengths[0]
    )
    branch, far_gu, far_dw = lax.optimization_barrier((branch, far_gu, far_dw))
    gate_up_all = jnp.concatenate([own_gu, far_gu, side_gu, swap(far_gu, 1)], axis=1)
    down_all = jnp.concatenate([own_dw, far_dw, side_dw, swap(far_dw, 1)], axis=0)
    carried = tokens.astype(jnp.float32) + 0.22 * branch
    normed = rms_scale(carried, norm_expert).astype(jnp.bfloat16)
    rows, width = normed.shape
    part = width // 2
    capacity = CAPACITY
    hits = routes[:, :, None] == jnp.arange(EXPERTS, dtype=jnp.int32)[None, None, :]
    marks = jnp.any(hits, axis=1)
    weight = jnp.sum(jnp.where(hits, gates[:, :, None], 0.0), axis=1)
    lower = (
        jnp.arange(rows, dtype=jnp.int32)[:, None] > jnp.arange(rows, dtype=jnp.int32)[None, :]
    ).astype(jnp.bfloat16)
    before = jnp.dot(lower, marks.astype(jnp.bfloat16), preferred_element_type=jnp.float32)
    slot = before.astype(jnp.int32)
    pick = marks[:, :, None] & (
        slot[:, :, None] == jnp.arange(capacity, dtype=jnp.int32)[None, None, :]
    )
    empty = jnp.zeros_like(pick)
    pick_lo = jnp.concatenate([pick, empty], axis=2).astype(jnp.bfloat16)
    pick_hi = jnp.concatenate([empty, pick], axis=2).astype(jnp.bfloat16)
    outgoing = jnp.einsum(
        "ter,tw->erw", pick_lo, normed[:, :part], preferred_element_type=jnp.float32
    ) + jnp.einsum("ter,tw->erw", pick_hi, normed[:, part:], preferred_element_type=jnp.float32)
    received = lax.all_to_all(
        outgoing.astype(jnp.bfloat16), ("req", "h"), split_axis=0, concat_axis=0, tiled=True
    )
    joined = jnp.concatenate([received[:, :capacity], received[:, capacity:]], axis=2)
    pieces = gate_up_all.reshape(gate_up_all.shape[0], slices, 2 * width_dev)
    gate_cols = pieces[..., :width_dev].reshape(gate_up_all.shape[0], slices * width_dev)
    up_cols = pieces[..., width_dev:].reshape(gate_up_all.shape[0], slices * width_dev)
    gate = jnp.einsum("scw,wh->sch", joined, gate_cols, preferred_element_type=jnp.float32)
    upper = jnp.einsum("scw,wh->sch", joined, up_cols, preferred_element_type=jnp.float32)
    hidden = (jax.nn.silu(gate) * upper).astype(jnp.bfloat16)
    produced = jnp.einsum(
        "sch,hw->scw", hidden, down_all, preferred_element_type=jnp.float32
    ).astype(jnp.bfloat16)
    back = jnp.concatenate([produced[..., :part], produced[..., part:]], axis=1)
    results = lax.all_to_all(back, ("req", "h"), split_axis=0, concat_axis=0, tiled=True)
    scale = jnp.where(pick, weight[:, :, None], 0.0)
    scale_hi = scale.astype(jnp.bfloat16)
    scale_lo = (scale - scale_hi.astype(jnp.float32)).astype(jnp.bfloat16)
    zero = jnp.zeros_like(scale_hi)

    def combine(lead, trail):
        low = jnp.concatenate([lead, zero], axis=2)
        high = jnp.concatenate([zero, lead], axis=2)
        low_t = jnp.concatenate([trail, zero], axis=2)
        high_t = jnp.concatenate([zero, trail], axis=2)
        first = jnp.einsum("ter,erw->tw", low, results, preferred_element_type=jnp.float32)
        first = first + jnp.einsum("ter,erw->tw", low_t, results, preferred_element_type=jnp.float32)
        second = jnp.einsum("ter,erw->tw", high, results, preferred_element_type=jnp.float32)
        second = second + jnp.einsum(
            "ter,erw->tw", high_t, results, preferred_element_type=jnp.float32
        )
        return jnp.concatenate([first, second], axis=1)

    mix = combine(scale_hi, scale_lo)
    return (branch.astype(jnp.bfloat16), mix.astype(jnp.bfloat16))


def solution(mesh):
    groups = mesh.shape["req"]
    slices = groups * mesh.shape["cuts"] // EXPERTS
    split = jax.sharding.Mesh(
        mesh.devices.reshape(groups, mesh.shape["cuts"] // slices, slices), ("req", "h", "q")
    )
    rows = ("req", "h", "q")
    placed = (
        P(rows, None),
        P(),
        P(),
        P(),
        P(),
        P(rows, None, None),
        P(rows, None, None),
        P(rows),
        P(rows, None),
        P(rows, None),
        P(rows, None, None),
        P(rows, None, None),
    )
    return jax.shard_map(
        on_device,
        mesh=split,
        in_specs=placed,
        out_specs=(P(rows, None), P(rows, None)),
        check_vma=False,
    )
```

```python
import jax
import jax.numpy as jnp
from jax import lax
from jax.sharding import PartitionSpec as P
from jax.experimental import pallas as pl
from jax.experimental.pallas import tpu as pltpu

HEADS = 16
KV_HEADS = 8
HEAD = 64
EXPERTS = 32
TOP = 8
CAPACITY = 40


def rms_scale(values, gain):
    wide = values.astype(jnp.float32)
    power = jnp.mean(wide * wide, axis=-1, keepdims=True)
    return wide * lax.rsqrt(power + 1e-06) * gain


def rotate(vectors, places):
    half = vectors.shape[-1] // 2
    freq = 10000.0 ** (-jnp.arange(half, dtype=jnp.float32) / half)
    angle = places[:, None] * freq[None, :]
    cosine = jnp.cos(angle)[:, None, :]
    sine = jnp.sin(angle)[:, None, :]
    first = vectors[..., :half]
    second = vectors[..., half:]
    return jnp.concatenate(
        [first * cosine - second * sine, second * cosine + first * sine], axis=-1
    )


def turn(values, cosine, sine, lead, half):
    partner = jnp.where(
        lead, pltpu.roll(values, values.shape[1] - half, 1), pltpu.roll(values, half, 1)
    )
    return jnp.where(lead, values * cosine - partner * sine, values * cosine + partner * sine)


def attention_kernel(length_ref, q_ref, k_ref, v_ref, cos_ref, sin_ref, kc_ref, vc_ref, o_ref):
    length = length_ref[0]
    span, lanes = kc_ref.shape
    rows = k_ref.shape[0]
    half = lanes // 2
    quarter = HEAD // 2
    cosine = cos_ref[...]
    sine = sin_ref[...]
    lane = lax.broadcasted_iota(jnp.int32, (rows, lanes), 1)
    lead = lane % HEAD < quarter
    low = lane < half
    kc = kc_ref[...]
    vc = vc_ref[...]
    kn = turn(k_ref[...], cosine, sine, lead, quarter).astype(jnp.bfloat16)
    vn = v_ref[...].astype(jnp.bfloat16)
    column = lax.broadcasted_iota(jnp.int32, (rows, span), 1)
    cache_ok = column < length
    new_col = lax.broadcasted_iota(jnp.int32, (rows, rows), 1)
    new_row = lax.broadcasted_iota(jnp.int32, (rows, rows), 0)
    new_ok = new_col <= new_row

    def scaled(values):
        rotated = turn(values, cosine, sine, lead, quarter).astype(jnp.bfloat16)
        return (rotated * 0.015625).astype(jnp.bfloat16).astype(jnp.float32)

    first = scaled(q_ref[:, :lanes])
    second = scaled(q_ref[:, lanes:])
    queries = (
        jnp.where(low, first, 0.0),
        jnp.where(low, pltpu.roll(first, half, 1), 0.0),
        jnp.where(low, 0.0, pltpu.roll(second, half, 1)),
        jnp.where(low, 0.0, second),
    )
    contract = (((1,), (1,)), ((), ()))
    outs = []
    for q in queries:
        q = q.astype(jnp.bfloat16)
        s = lax.dot_general(q, kc, contract, preferred_element_type=jnp.float32)
        s = jnp.where(cache_ok, s, -1e30)
        sn = lax.dot_general(q, kn, contract, preferred_element_type=jnp.float32)
        sn = jnp.where(new_ok, sn, -1e30)
        top = jnp.maximum(jnp.max(s, axis=1, keepdims=True), jnp.max(sn, axis=1, keepdims=True))
        e = jnp.exp(s - top)
        en = jnp.exp(sn - top)
        total = jnp.sum(e, axis=1, keepdims=True) + jnp.sum(en, axis=1, keepdims=True)
        inverse = 1.0 / total
        w = (e * inverse).astype(jnp.bfloat16)
        wn = (en * inverse).astype(jnp.bfloat16)
        o = jnp.dot(w, vc, preferred_element_type=jnp.float32) + jnp.dot(
            wn, vn, preferred_element_type=jnp.float32
        )
        outs.append(o.astype(jnp.bfloat16).astype(jnp.float32))
    left = jnp.where(low, outs[0], pltpu.roll(outs[1], half, 1))
    right = jnp.where(low, pltpu.roll(outs[2], half, 1), outs[3])
    o_ref[:, :lanes] = left.astype(jnp.bfloat16)
    o_ref[:, lanes:] = right.astype(jnp.bfloat16)


def attention_core(length, mixed, cosine, sine, kc, vc, interpret=False):
    rows = mixed.shape[0]
    span, kvwidth = kc.shape
    qwidth = HEADS * HEAD
    lanes = 2 * HEAD
    pairs = kvwidth // lanes
    qblock = qwidth // pairs
    kstart = qwidth // lanes
    vstart = kstart + pairs
    return pl.pallas_call(
        attention_kernel,
        grid_spec=pltpu.PrefetchScalarGridSpec(
            num_scalar_prefetch=1,
            grid=(pairs,),
            in_specs=[
                pl.BlockSpec((rows, qblock), lambda p, n: (0, p)),
                pl.BlockSpec((rows, lanes), lambda p, n: (0, kstart + p)),
                pl.BlockSpec((rows, lanes), lambda p, n: (0, vstart + p)),
                pl.BlockSpec((rows, lanes), lambda p, n: (0, 0)),
                pl.BlockSpec((rows, lanes), lambda p, n: (0, 0)),
                pl.BlockSpec((span, lanes), lambda p, n: (0, p)),
                pl.BlockSpec((span, lanes), lambda p, n: (0, p)),
            ],
            out_specs=pl.BlockSpec((rows, qblock), lambda p, n: (0, p)),
        ),
        out_shape=jax.ShapeDtypeStruct((rows, qwidth), jnp.bfloat16),
        interpret=interpret,
    )(length, mixed, mixed, mixed, cosine, sine, kc, vc)


def attend(tokens, qkv_weight, out_weight, norm_attn, keys_cache, values_cache, length, interpret=False):
    rows = tokens.shape[0]
    half = HEAD // 2
    normed = rms_scale(tokens, norm_attn).astype(jnp.bfloat16)
    mixed = jnp.dot(normed, qkv_weight, preferred_element_type=jnp.float32)
    places = (length + jnp.arange(rows, dtype=jnp.int32)).astype(jnp.float32)
    freq = 10000.0 ** (-jnp.arange(half, dtype=jnp.float32) / half)
    angle = places[:, None] * freq[None, :]
    cosine = jnp.tile(jnp.cos(angle), (1, 4))
    sine = jnp.tile(jnp.sin(angle), (1, 4))
    heads_out = attention_core(
        length.reshape(1).astype(jnp.int32),
        mixed,
        cosine,
        sine,
        keys_cache,
        values_cache,
        interpret=interpret,
    )
    return jnp.dot(heads_out, out_weight, preferred_element_type=jnp.float32)


def swap(piece, bit):
    return lax.ppermute(piece, "q", [(i, i ^ bit) for i in range(lax.axis_size("q"))])


def on_device(
    tokens,
    qkv_weight,
    out_weight,
    norm_attn,
    norm_expert,
    keys_cache,
    values_cache,
    lengths,
    routes,
    gates,
    gate_up,
    down_weight,
):
    slices = lax.axis_size("q")
    width_dev = down_weight.shape[1]
    own_gu = gate_up[0]
    own_dw = down_weight[0]
    far_gu = swap(own_gu, 2)
    far_dw = swap(own_dw, 2)
    side_gu = swap(own_gu, 1)
    side_dw = swap(own_dw, 1)
    branch = attend(
        tokens, qkv_weight, out_weight, norm_attn, keys_cache[0], values_cache[0], lengths[0]
    )
    branch, far_gu, far_dw = lax.optimization_barrier((branch, far_gu, far_dw))
    gate_up_all = jnp.concatenate([own_gu, far_gu, side_gu, swap(far_gu, 1)], axis=1)
    down_all = jnp.concatenate([own_dw, far_dw, side_dw, swap(far_dw, 1)], axis=0)
    carried = tokens.astype(jnp.float32) + 0.22 * branch
    normed = rms_scale(carried, norm_expert).astype(jnp.bfloat16)
    rows, width = normed.shape
    part = width // 2
    capacity = CAPACITY
    hits = routes[:, :, None] == jnp.arange(EXPERTS, dtype=jnp.int32)[None, None, :]
    marks = jnp.any(hits, axis=1)
    weight = jnp.sum(jnp.where(hits, gates[:, :, None], 0.0), axis=1)
    lower = (
        jnp.arange(rows, dtype=jnp.int32)[:, None] > jnp.arange(rows, dtype=jnp.int32)[None, :]
    ).astype(jnp.bfloat16)
    before = jnp.dot(lower, marks.astype(jnp.bfloat16), preferred_element_type=jnp.float32)
    slot = before.astype(jnp.int32)
    pick = marks[:, :, None] & (
        slot[:, :, None] == jnp.arange(capacity, dtype=jnp.int32)[None, None, :]
    )
    empty = jnp.zeros_like(pick)
    pick_lo = jnp.concatenate([pick, empty], axis=2).astype(jnp.bfloat16)
    pick_hi = jnp.concatenate([empty, pick], axis=2).astype(jnp.bfloat16)
    outgoing = jnp.einsum(
        "ter,tw->erw", pick_lo, normed[:, :part], preferred_element_type=jnp.float32
    ) + jnp.einsum("ter,tw->erw", pick_hi, normed[:, part:], preferred_element_type=jnp.float32)
    received = lax.all_to_all(
        outgoing.astype(jnp.bfloat16), ("req", "h"), split_axis=0, concat_axis=0, tiled=True
    )
    joined = jnp.concatenate([received[:, :capacity], received[:, capacity:]], axis=2)
    pieces = gate_up_all.reshape(gate_up_all.shape[0], slices, 2 * width_dev)
    gate_cols = pieces[..., :width_dev].reshape(gate_up_all.shape[0], slices * width_dev)
    up_cols = pieces[..., width_dev:].reshape(gate_up_all.shape[0], slices * width_dev)
    gate = jnp.einsum("scw,wh->sch", joined, gate_cols, preferred_element_type=jnp.float32)
    upper = jnp.einsum("scw,wh->sch", joined, up_cols, preferred_element_type=jnp.float32)
    hidden = (jax.nn.silu(gate) * upper).astype(jnp.bfloat16)
    produced = jnp.einsum(
        "sch,hw->scw", hidden, down_all, preferred_element_type=jnp.float32
    ).astype(jnp.bfloat16)
    back = jnp.concatenate([produced[..., :part], produced[..., part:]], axis=1)
    results = lax.all_to_all(back, ("req", "h"), split_axis=0, concat_axis=0, tiled=True)
    scale = jnp.where(pick, weight[:, :, None], 0.0)
    output = jnp.concatenate([results[:, :capacity], results[:, capacity:]], axis=2)
    mix = jnp.einsum(
        "tec,ecw->tw",
        scale,
        output.astype(jnp.float32),
        precision=lax.Precision.HIGHEST,
        preferred_element_type=jnp.float32,
    )
    return (branch.astype(jnp.bfloat16), mix.astype(jnp.bfloat16))


def solution(mesh):
    groups = mesh.shape["req"]
    slices = groups * mesh.shape["cuts"] // EXPERTS
    split = jax.sharding.Mesh(
        mesh.devices.reshape(groups, mesh.shape["cuts"] // slices, slices), ("req", "h", "q")
    )
    rows = ("req", "h", "q")
    placed = (
        P(rows, None),
        P(),
        P(),
        P(),
        P(),
        P(rows, None, None),
        P(rows, None, None),
        P(rows),
        P(rows, None),
        P(rows, None),
        P(rows, None, None),
        P(rows, None, None),
    )
    return jax.shard_map(
        on_device,
        mesh=split,
        in_specs=placed,
        out_specs=(P(rows, None), P(rows, None)),
        check_vma=False,
    )
```

```python
import jax
import jax.numpy as jnp
from jax import lax
from jax.sharding import PartitionSpec as P
from jax.experimental import pallas as pl
from jax.experimental.pallas import tpu as pltpu

HEADS = 16
KV_HEADS = 8
HEAD = 64
EXPERTS = 32
TOP = 8
CAPACITY = 40


def rms_scale(values, gain):
    wide = values.astype(jnp.float32)
    power = jnp.mean(wide * wide, axis=-1, keepdims=True)
    return wide * lax.rsqrt(power + 1e-06) * gain


def rotate(vectors, places):
    half = vectors.shape[-1] // 2
    freq = 10000.0 ** (-jnp.arange(half, dtype=jnp.float32) / half)
    angle = places[:, None] * freq[None, :]
    cosine = jnp.cos(angle)[:, None, :]
    sine = jnp.sin(angle)[:, None, :]
    first = vectors[..., :half]
    second = vectors[..., half:]
    return jnp.concatenate(
        [first * cosine - second * sine, second * cosine + first * sine], axis=-1
    )


def turn(values, cosine, sine, lead, half):
    partner = jnp.where(
        lead, pltpu.roll(values, values.shape[1] - half, 1), pltpu.roll(values, half, 1)
    )
    return jnp.where(lead, values * cosine - partner * sine, values * cosine + partner * sine)


def attention_kernel(
    length_ref, q_ref, k_ref, v_ref, cos_ref, sin_ref, kc_ref, vc_ref, o_ref, s_ref, sn_ref, w_ref, wn_ref
):
    length = length_ref[0]
    span, lanes = kc_ref.shape
    rows = k_ref.shape[0]
    half = lanes // 2
    quarter = HEAD // 2
    cosine = cos_ref[...]
    sine = sin_ref[...]
    lane = lax.broadcasted_iota(jnp.int32, (rows, lanes), 1)
    lead = lane % HEAD < quarter
    low = lane < half
    kc = kc_ref[...]
    vc = vc_ref[...]
    kn = turn(k_ref[...], cosine, sine, lead, quarter).astype(jnp.bfloat16)
    vn = v_ref[...].astype(jnp.bfloat16)
    def scaled(values):
        rotated = turn(values, cosine, sine, lead, quarter).astype(jnp.bfloat16)
        return (rotated * 0.015625).astype(jnp.bfloat16).astype(jnp.float32)

    first = scaled(q_ref[:, :lanes])
    second = scaled(q_ref[:, lanes:])
    queries = (
        jnp.where(low, first, 0.0),
        jnp.where(low, pltpu.roll(first, half, 1), 0.0),
        jnp.where(low, 0.0, pltpu.roll(second, half, 1)),
        jnp.where(low, 0.0, second),
    )
    contract = (((1,), (1,)), ((), ()))
    chunk = 16
    outs = []
    for q in queries:
        q = q.astype(jnp.bfloat16)
        s_ref[...] = lax.dot_general(q, kc, contract, preferred_element_type=jnp.float32)
        sn_ref[...] = lax.dot_general(q, kn, contract, preferred_element_type=jnp.float32)

        def normalize(i, carry):
            at = pl.ds(pl.multiple_of(i * chunk, chunk), chunk)
            column = lax.broadcasted_iota(jnp.int32, (chunk, span), 1)
            s = jnp.where(column < length, s_ref[at, :], -1e30)
            new_col = lax.broadcasted_iota(jnp.int32, (chunk, rows), 1)
            new_row = lax.broadcasted_iota(jnp.int32, (chunk, rows), 0) + i * chunk
            sn = jnp.where(new_col <= new_row, sn_ref[at, :], -1e30)
            top = jnp.maximum(
                jnp.max(s, axis=1, keepdims=True), jnp.max(sn, axis=1, keepdims=True)
            )
            e = jnp.exp(s - top)
            en = jnp.exp(sn - top)
            total = jnp.sum(e, axis=1, keepdims=True) + jnp.sum(en, axis=1, keepdims=True)
            inverse = 1.0 / total
            w_ref[at, :] = (e * inverse).astype(jnp.bfloat16)
            wn_ref[at, :] = (en * inverse).astype(jnp.bfloat16)
            return carry

        lax.fori_loop(0, rows // chunk, normalize, 0)
        o = jnp.dot(w_ref[...], vc, preferred_element_type=jnp.float32) + jnp.dot(
            wn_ref[...], vn, preferred_element_type=jnp.float32
        )
        outs.append(o.astype(jnp.bfloat16).astype(jnp.float32))
    left = jnp.where(low, outs[0], pltpu.roll(outs[1], half, 1))
    right = jnp.where(low, pltpu.roll(outs[2], half, 1), outs[3])
    o_ref[:, :lanes] = left.astype(jnp.bfloat16)
    o_ref[:, lanes:] = right.astype(jnp.bfloat16)


def attention_core(length, mixed, cosine, sine, kc, vc, interpret=False):
    rows = mixed.shape[0]
    span, kvwidth = kc.shape
    qwidth = HEADS * HEAD
    lanes = 2 * HEAD
    pairs = kvwidth // lanes
    qblock = qwidth // pairs
    kstart = qwidth // lanes
    vstart = kstart + pairs
    return pl.pallas_call(
        attention_kernel,
        grid_spec=pltpu.PrefetchScalarGridSpec(
            num_scalar_prefetch=1,
            grid=(pairs,),
            in_specs=[
                pl.BlockSpec((rows, qblock), lambda p, n: (0, p)),
                pl.BlockSpec((rows, lanes), lambda p, n: (0, kstart + p)),
                pl.BlockSpec((rows, lanes), lambda p, n: (0, vstart + p)),
                pl.BlockSpec((rows, lanes), lambda p, n: (0, 0)),
                pl.BlockSpec((rows, lanes), lambda p, n: (0, 0)),
                pl.BlockSpec((span, lanes), lambda p, n: (0, p)),
                pl.BlockSpec((span, lanes), lambda p, n: (0, p)),
            ],
            out_specs=pl.BlockSpec((rows, qblock), lambda p, n: (0, p)),
            scratch_shapes=[
                pltpu.VMEM((rows, span), jnp.float32),
                pltpu.VMEM((rows, rows), jnp.float32),
                pltpu.VMEM((rows, span), jnp.bfloat16),
                pltpu.VMEM((rows, rows), jnp.bfloat16),
            ],
        ),
        out_shape=jax.ShapeDtypeStruct((rows, qwidth), jnp.bfloat16),
        interpret=interpret,
    )(length, mixed, mixed, mixed, cosine, sine, kc, vc)


def attend(tokens, qkv_weight, out_weight, norm_attn, keys_cache, values_cache, length, interpret=False):
    rows = tokens.shape[0]
    half = HEAD // 2
    normed = rms_scale(tokens, norm_attn).astype(jnp.bfloat16)
    mixed = jnp.dot(normed, qkv_weight, preferred_element_type=jnp.float32)
    places = (length + jnp.arange(rows, dtype=jnp.int32)).astype(jnp.float32)
    freq = 10000.0 ** (-jnp.arange(half, dtype=jnp.float32) / half)
    angle = places[:, None] * freq[None, :]
    cosine = jnp.tile(jnp.cos(angle), (1, 4))
    sine = jnp.tile(jnp.sin(angle), (1, 4))
    heads_out = attention_core(
        length.reshape(1).astype(jnp.int32),
        mixed,
        cosine,
        sine,
        keys_cache,
        values_cache,
        interpret=interpret,
    )
    return jnp.dot(heads_out, out_weight, preferred_element_type=jnp.float32)


def swap(piece, bit):
    return lax.ppermute(piece, "q", [(i, i ^ bit) for i in range(lax.axis_size("q"))])


def on_device(
    tokens,
    qkv_weight,
    out_weight,
    norm_attn,
    norm_expert,
    keys_cache,
    values_cache,
    lengths,
    routes,
    gates,
    gate_up,
    down_weight,
):
    slices = lax.axis_size("q")
    width_dev = down_weight.shape[1]
    own_gu = gate_up[0]
    own_dw = down_weight[0]
    far_gu = swap(own_gu, 2)
    far_dw = swap(own_dw, 2)
    side_gu = swap(own_gu, 1)
    side_dw = swap(own_dw, 1)
    branch = attend(
        tokens, qkv_weight, out_weight, norm_attn, keys_cache[0], values_cache[0], lengths[0]
    )
    branch, far_gu, far_dw = lax.optimization_barrier((branch, far_gu, far_dw))
    gate_up_all = jnp.concatenate([own_gu, far_gu, side_gu, swap(far_gu, 1)], axis=1)
    down_all = jnp.concatenate([own_dw, far_dw, side_dw, swap(far_dw, 1)], axis=0)
    carried = tokens.astype(jnp.float32) + 0.22 * branch
    normed = rms_scale(carried, norm_expert).astype(jnp.bfloat16)
    rows, width = normed.shape
    part = width // 2
    capacity = CAPACITY
    hits = routes[:, :, None] == jnp.arange(EXPERTS, dtype=jnp.int32)[None, None, :]
    marks = jnp.any(hits, axis=1)
    weight = jnp.sum(jnp.where(hits, gates[:, :, None], 0.0), axis=1)
    lower = (
        jnp.arange(rows, dtype=jnp.int32)[:, None] > jnp.arange(rows, dtype=jnp.int32)[None, :]
    ).astype(jnp.bfloat16)
    before = jnp.dot(lower, marks.astype(jnp.bfloat16), preferred_element_type=jnp.float32)
    slot = before.astype(jnp.int32)
    pick = marks[:, :, None] & (
        slot[:, :, None] == jnp.arange(capacity, dtype=jnp.int32)[None, None, :]
    )
    empty = jnp.zeros_like(pick)
    pick_lo = jnp.concatenate([pick, empty], axis=2).astype(jnp.bfloat16)
    pick_hi = jnp.concatenate([empty, pick], axis=2).astype(jnp.bfloat16)
    outgoing = jnp.einsum(
        "ter,tw->erw", pick_lo, normed[:, :part], preferred_element_type=jnp.float32
    ) + jnp.einsum("ter,tw->erw", pick_hi, normed[:, part:], preferred_element_type=jnp.float32)
    received = lax.all_to_all(
        outgoing.astype(jnp.bfloat16), ("req", "h"), split_axis=0, concat_axis=0, tiled=True
    )
    joined = jnp.concatenate([received[:, :capacity], received[:, capacity:]], axis=2)
    pieces = gate_up_all.reshape(gate_up_all.shape[0], slices, 2 * width_dev)
    gate_cols = pieces[..., :width_dev].reshape(gate_up_all.shape[0], slices * width_dev)
    up_cols = pieces[..., width_dev:].reshape(gate_up_all.shape[0], slices * width_dev)
    gate = jnp.einsum("scw,wh->sch", joined, gate_cols, preferred_element_type=jnp.float32)
    upper = jnp.einsum("scw,wh->sch", joined, up_cols, preferred_element_type=jnp.float32)
    hidden = (jax.nn.silu(gate) * upper).astype(jnp.bfloat16)
    produced = jnp.einsum(
        "sch,hw->scw", hidden, down_all, preferred_element_type=jnp.float32
    ).astype(jnp.bfloat16)
    back = jnp.concatenate([produced[..., :part], produced[..., part:]], axis=1)
    results = lax.all_to_all(back, ("req", "h"), split_axis=0, concat_axis=0, tiled=True)
    scale = jnp.where(pick, weight[:, :, None], 0.0)
    output = jnp.concatenate([results[:, :capacity], results[:, capacity:]], axis=2)
    mix = jnp.einsum(
        "tec,ecw->tw",
        scale,
        output.astype(jnp.float32),
        precision=lax.Precision.HIGHEST,
        preferred_element_type=jnp.float32,
    )
    return (branch.astype(jnp.bfloat16), mix.astype(jnp.bfloat16))


def solution(mesh):
    groups = mesh.shape["req"]
    slices = groups * mesh.shape["cuts"] // EXPERTS
    split = jax.sharding.Mesh(
        mesh.devices.reshape(groups, mesh.shape["cuts"] // slices, slices), ("req", "h", "q")
    )
    rows = ("req", "h", "q")
    placed = (
        P(rows, None),
        P(),
        P(),
        P(),
        P(),
        P(rows, None, None),
        P(rows, None, None),
        P(rows),
        P(rows, None),
        P(rows, None),
        P(rows, None, None),
        P(rows, None, None),
    )
    return jax.shard_map(
        on_device,
        mesh=split,
        in_specs=placed,
        out_specs=(P(rows, None), P(rows, None)),
        check_vma=False,
    )
```

```python
import jax
import jax.numpy as jnp
from jax import lax
from jax.sharding import PartitionSpec as P
from jax.experimental import pallas as pl
from jax.experimental.pallas import tpu as pltpu

HEADS = 16
KV_HEADS = 8
HEAD = 64
EXPERTS = 32
TOP = 8
CAPACITY = 40


def rms_scale(values, gain):
    wide = values.astype(jnp.float32)
    power = jnp.mean(wide * wide, axis=-1, keepdims=True)
    return wide * lax.rsqrt(power + 1e-06) * gain


def rotate(vectors, places):
    half = vectors.shape[-1] // 2
    freq = 10000.0 ** (-jnp.arange(half, dtype=jnp.float32) / half)
    angle = places[:, None] * freq[None, :]
    cosine = jnp.cos(angle)[:, None, :]
    sine = jnp.sin(angle)[:, None, :]
    first = vectors[..., :half]
    second = vectors[..., half:]
    return jnp.concatenate(
        [first * cosine - second * sine, second * cosine + first * sine], axis=-1
    )


def turn(values, cosine, sine, lead, half):
    partner = jnp.where(
        lead, pltpu.roll(values, values.shape[1] - half, 1), pltpu.roll(values, half, 1)
    )
    return jnp.where(lead, values * cosine - partner * sine, values * cosine + partner * sine)


def attention_kernel(length_ref, q_ref, k_ref, v_ref, cos_ref, sin_ref, kc_ref, vc_ref, o_ref):
    length = length_ref[0]
    span, lanes = kc_ref.shape
    rows = k_ref.shape[0]
    half = lanes // 2
    quarter = HEAD // 2
    cosine = cos_ref[...]
    sine = sin_ref[...]
    lane = lax.broadcasted_iota(jnp.int32, (rows, lanes), 1)
    lead = lane % HEAD < quarter
    low = lane < half
    kc = kc_ref[...]
    vc = vc_ref[...]
    kn = turn(k_ref[...], cosine, sine, lead, quarter).astype(jnp.bfloat16)
    vn = v_ref[...].astype(jnp.bfloat16)
    def scaled(values):
        rotated = turn(values, cosine, sine, lead, quarter).astype(jnp.bfloat16)
        return (rotated * 0.015625).astype(jnp.bfloat16).astype(jnp.float32)

    first = scaled(q_ref[:, :lanes])
    second = scaled(q_ref[:, lanes:])
    queries = (
        jnp.where(low, first, 0.0),
        jnp.where(low, pltpu.roll(first, half, 1), 0.0),
        jnp.where(low, 0.0, pltpu.roll(second, half, 1)),
        jnp.where(low, 0.0, second),
    )
    contract = (((1,), (1,)), ((), ()))
    stacked = jnp.concatenate(queries, axis=0).astype(jnp.bfloat16)
    tall = stacked.shape[0]
    column = lax.broadcasted_iota(jnp.int32, (tall, span), 1)
    cache_ok = column < length
    new_col = lax.broadcasted_iota(jnp.int32, (tall, rows), 1)
    new_row = lax.broadcasted_iota(jnp.int32, (tall, rows), 0) % rows
    new_ok = new_col <= new_row
    s = lax.dot_general(stacked, kc, contract, preferred_element_type=jnp.float32)
    s = jnp.where(cache_ok, s, -1e30)
    sn = lax.dot_general(stacked, kn, contract, preferred_element_type=jnp.float32)
    sn = jnp.where(new_ok, sn, -1e30)
    top = jnp.maximum(jnp.max(s, axis=1, keepdims=True), jnp.max(sn, axis=1, keepdims=True))
    e = jnp.exp(s - top)
    en = jnp.exp(sn - top)
    total = jnp.sum(e, axis=1, keepdims=True) + jnp.sum(en, axis=1, keepdims=True)
    inverse = 1.0 / total
    w = (e * inverse).astype(jnp.bfloat16)
    wn = (en * inverse).astype(jnp.bfloat16)
    o = jnp.dot(w, vc, preferred_element_type=jnp.float32) + jnp.dot(
        wn, vn, preferred_element_type=jnp.float32
    )
    o = o.astype(jnp.bfloat16).astype(jnp.float32)
    outs = [o[j * rows : (j + 1) * rows] for j in range(len(queries))]
    left = jnp.where(low, outs[0], pltpu.roll(outs[1], half, 1))
    right = jnp.where(low, pltpu.roll(outs[2], half, 1), outs[3])
    o_ref[:, :lanes] = left.astype(jnp.bfloat16)
    o_ref[:, lanes:] = right.astype(jnp.bfloat16)


def attention_core(length, mixed, cosine, sine, kc, vc, interpret=False):
    rows = mixed.shape[0]
    span, kvwidth = kc.shape
    qwidth = HEADS * HEAD
    lanes = 2 * HEAD
    pairs = kvwidth // lanes
    qblock = qwidth // pairs
    kstart = qwidth // lanes
    vstart = kstart + pairs
    return pl.pallas_call(
        attention_kernel,
        grid_spec=pltpu.PrefetchScalarGridSpec(
            num_scalar_prefetch=1,
            grid=(pairs,),
            in_specs=[
                pl.BlockSpec((rows, qblock), lambda p, n: (0, p)),
                pl.BlockSpec((rows, lanes), lambda p, n: (0, kstart + p)),
                pl.BlockSpec((rows, lanes), lambda p, n: (0, vstart + p)),
                pl.BlockSpec((rows, lanes), lambda p, n: (0, 0)),
                pl.BlockSpec((rows, lanes), lambda p, n: (0, 0)),
                pl.BlockSpec((span, lanes), lambda p, n: (0, p)),
                pl.BlockSpec((span, lanes), lambda p, n: (0, p)),
            ],
            out_specs=pl.BlockSpec((rows, qblock), lambda p, n: (0, p)),
        ),
        out_shape=jax.ShapeDtypeStruct((rows, qwidth), jnp.bfloat16),
        interpret=interpret,
    )(length, mixed, mixed, mixed, cosine, sine, kc, vc)


def attend(tokens, qkv_weight, out_weight, norm_attn, keys_cache, values_cache, length, interpret=False):
    rows = tokens.shape[0]
    half = HEAD // 2
    normed = rms_scale(tokens, norm_attn).astype(jnp.bfloat16)
    mixed = jnp.dot(normed, qkv_weight, preferred_element_type=jnp.float32)
    places = (length + jnp.arange(rows, dtype=jnp.int32)).astype(jnp.float32)
    freq = 10000.0 ** (-jnp.arange(half, dtype=jnp.float32) / half)
    angle = places[:, None] * freq[None, :]
    cosine = jnp.tile(jnp.cos(angle), (1, 4))
    sine = jnp.tile(jnp.sin(angle), (1, 4))
    heads_out = attention_core(
        length.reshape(1).astype(jnp.int32),
        mixed,
        cosine,
        sine,
        keys_cache,
        values_cache,
        interpret=interpret,
    )
    return jnp.dot(heads_out, out_weight, preferred_element_type=jnp.float32)


def swap(piece, bit):
    return lax.ppermute(piece, "q", [(i, i ^ bit) for i in range(lax.axis_size("q"))])


def on_device(
    tokens,
    qkv_weight,
    out_weight,
    norm_attn,
    norm_expert,
    keys_cache,
    values_cache,
    lengths,
    routes,
    gates,
    gate_up,
    down_weight,
):
    slices = lax.axis_size("q")
    width_dev = down_weight.shape[1]
    own_gu = gate_up[0]
    own_dw = down_weight[0]
    far_gu = swap(own_gu, 2)
    far_dw = swap(own_dw, 2)
    side_gu = swap(own_gu, 1)
    side_dw = swap(own_dw, 1)
    branch = attend(
        tokens, qkv_weight, out_weight, norm_attn, keys_cache[0], values_cache[0], lengths[0]
    )
    branch, far_gu, far_dw = lax.optimization_barrier((branch, far_gu, far_dw))
    gate_up_all = jnp.concatenate([own_gu, far_gu, side_gu, swap(far_gu, 1)], axis=1)
    down_all = jnp.concatenate([own_dw, far_dw, side_dw, swap(far_dw, 1)], axis=0)
    carried = tokens.astype(jnp.float32) + 0.22 * branch
    normed = rms_scale(carried, norm_expert).astype(jnp.bfloat16)
    rows, width = normed.shape
    part = width // 2
    capacity = CAPACITY
    hits = routes[:, :, None] == jnp.arange(EXPERTS, dtype=jnp.int32)[None, None, :]
    marks = jnp.any(hits, axis=1)
    weight = jnp.sum(jnp.where(hits, gates[:, :, None], 0.0), axis=1)
    lower = (
        jnp.arange(rows, dtype=jnp.int32)[:, None] > jnp.arange(rows, dtype=jnp.int32)[None, :]
    ).astype(jnp.bfloat16)
    before = jnp.dot(lower, marks.astype(jnp.bfloat16), preferred_element_type=jnp.float32)
    slot = before.astype(jnp.int32)
    pick = marks[:, :, None] & (
        slot[:, :, None] == jnp.arange(capacity, dtype=jnp.int32)[None, None, :]
    )
    empty = jnp.zeros_like(pick)
    pick_lo = jnp.concatenate([pick, empty], axis=2).astype(jnp.bfloat16)
    pick_hi = jnp.concatenate([empty, pick], axis=2).astype(jnp.bfloat16)
    outgoing = jnp.einsum(
        "ter,tw->erw", pick_lo, normed[:, :part], preferred_element_type=jnp.float32
    ) + jnp.einsum("ter,tw->erw", pick_hi, normed[:, part:], preferred_element_type=jnp.float32)
    received = lax.all_to_all(
        outgoing.astype(jnp.bfloat16), ("req", "h"), split_axis=0, concat_axis=0, tiled=True
    )
    joined = jnp.concatenate([received[:, :capacity], received[:, capacity:]], axis=2)
    pieces = gate_up_all.reshape(gate_up_all.shape[0], slices, 2 * width_dev)
    gate_cols = pieces[..., :width_dev].reshape(gate_up_all.shape[0], slices * width_dev)
    up_cols = pieces[..., width_dev:].reshape(gate_up_all.shape[0], slices * width_dev)
    gate = jnp.einsum("scw,wh->sch", joined, gate_cols, preferred_element_type=jnp.float32)
    upper = jnp.einsum("scw,wh->sch", joined, up_cols, preferred_element_type=jnp.float32)
    hidden = (jax.nn.silu(gate) * upper).astype(jnp.bfloat16)
    produced = jnp.einsum(
        "sch,hw->scw", hidden, down_all, preferred_element_type=jnp.float32
    ).astype(jnp.bfloat16)
    back = jnp.concatenate([produced[..., :part], produced[..., part:]], axis=1)
    results = lax.all_to_all(back, ("req", "h"), split_axis=0, concat_axis=0, tiled=True)
    scale = jnp.where(pick, weight[:, :, None], 0.0)
    output = jnp.concatenate([results[:, :capacity], results[:, capacity:]], axis=2)
    mix = jnp.einsum(
        "tec,ecw->tw",
        scale,
        output.astype(jnp.float32),
        precision=lax.Precision.HIGHEST,
        preferred_element_type=jnp.float32,
    )
    return (branch.astype(jnp.bfloat16), mix.astype(jnp.bfloat16))


def solution(mesh):
    groups = mesh.shape["req"]
    slices = groups * mesh.shape["cuts"] // EXPERTS
    split = jax.sharding.Mesh(
        mesh.devices.reshape(groups, mesh.shape["cuts"] // slices, slices), ("req", "h", "q")
    )
    rows = ("req", "h", "q")
    placed = (
        P(rows, None),
        P(),
        P(),
        P(),
        P(),
        P(rows, None, None),
        P(rows, None, None),
        P(rows),
        P(rows, None),
        P(rows, None),
        P(rows, None, None),
        P(rows, None, None),
    )
    return jax.shard_map(
        on_device,
        mesh=split,
        in_specs=placed,
        out_specs=(P(rows, None), P(rows, None)),
        check_vma=False,
    )
```

```python
import jax
import jax.numpy as jnp
from jax import lax
from jax.sharding import PartitionSpec as P
from jax.experimental import pallas as pl
from jax.experimental.pallas import tpu as pltpu

HEADS = 16
KV_HEADS = 8
HEAD = 64
EXPERTS = 32
TOP = 8
CAPACITY = 40


def rms_scale(values, gain):
    wide = values.astype(jnp.float32)
    power = jnp.mean(wide * wide, axis=-1, keepdims=True)
    return wide * lax.rsqrt(power + 1e-06) * gain


def rotate(vectors, places):
    half = vectors.shape[-1] // 2
    freq = 10000.0 ** (-jnp.arange(half, dtype=jnp.float32) / half)
    angle = places[:, None] * freq[None, :]
    cosine = jnp.cos(angle)[:, None, :]
    sine = jnp.sin(angle)[:, None, :]
    first = vectors[..., :half]
    second = vectors[..., half:]
    return jnp.concatenate(
        [first * cosine - second * sine, second * cosine + first * sine], axis=-1
    )


def turn(values, cosine, sine, lead, half):
    partner = jnp.where(
        lead, pltpu.roll(values, values.shape[1] - half, 1), pltpu.roll(values, half, 1)
    )
    return jnp.where(lead, values * cosine - partner * sine, values * cosine + partner * sine)


def attention_kernel(length_ref, q_ref, k_ref, v_ref, cos_ref, sin_ref, kc_ref, vc_ref, o_ref):
    length = length_ref[0]
    span, lanes = kc_ref.shape
    rows = k_ref.shape[0]
    half = lanes // 2
    quarter = HEAD // 2
    cosine = cos_ref[...]
    sine = sin_ref[...]
    lane = lax.broadcasted_iota(jnp.int32, (rows, lanes), 1)
    lead = lane % HEAD < quarter
    low = lane < half
    kc = kc_ref[...]
    vc = vc_ref[...]
    kn = turn(k_ref[...], cosine, sine, lead, quarter).astype(jnp.bfloat16)
    vn = v_ref[...].astype(jnp.bfloat16)
    column = lax.broadcasted_iota(jnp.int32, (rows, span), 1)
    cache_ok = column < length
    new_col = lax.broadcasted_iota(jnp.int32, (rows, rows), 1)
    new_row = lax.broadcasted_iota(jnp.int32, (rows, rows), 0)
    new_ok = new_col <= new_row

    def scaled(values):
        rotated = turn(values, cosine, sine, lead, quarter).astype(jnp.bfloat16)
        return (rotated * 0.015625).astype(jnp.bfloat16).astype(jnp.float32)

    first = scaled(q_ref[:, :lanes])
    second = scaled(q_ref[:, lanes:])
    queries = (
        jnp.where(low, first, 0.0),
        jnp.where(low, pltpu.roll(first, half, 1), 0.0),
        jnp.where(low, 0.0, pltpu.roll(second, half, 1)),
        jnp.where(low, 0.0, second),
    )
    contract = (((1,), (1,)), ((), ()))
    outs = []
    for q in queries:
        q = q.astype(jnp.bfloat16)
        s = lax.dot_general(q, kc, contract, preferred_element_type=jnp.float32)
        s = jnp.where(cache_ok, s, -1e30)
        sn = lax.dot_general(q, kn, contract, preferred_element_type=jnp.float32)
        sn = jnp.where(new_ok, sn, -1e30)
        top = jnp.maximum(jnp.max(s, axis=1, keepdims=True), jnp.max(sn, axis=1, keepdims=True))
        e = jnp.exp(s - top)
        en = jnp.exp(sn - top)
        total = jnp.sum(e, axis=1, keepdims=True) + jnp.sum(en, axis=1, keepdims=True)
        inverse = 1.0 / total
        w = (e * inverse).astype(jnp.bfloat16)
        wn = (en * inverse).astype(jnp.bfloat16)
        o = jnp.dot(w, vc, preferred_element_type=jnp.float32) + jnp.dot(
            wn, vn, preferred_element_type=jnp.float32
        )
        outs.append(o.astype(jnp.bfloat16).astype(jnp.float32))
    left = jnp.where(low, outs[0], pltpu.roll(outs[1], half, 1))
    right = jnp.where(low, pltpu.roll(outs[2], half, 1), outs[3])
    o_ref[:, :lanes] = left.astype(jnp.bfloat16)
    o_ref[:, lanes:] = right.astype(jnp.bfloat16)


def attention_core(length, mixed, cosine, sine, kc, vc, interpret=False):
    rows = mixed.shape[0]
    span, kvwidth = kc.shape
    qwidth = HEADS * HEAD
    lanes = 2 * HEAD
    pairs = kvwidth // lanes
    qblock = qwidth // pairs
    kstart = qwidth // lanes
    vstart = kstart + pairs
    return pl.pallas_call(
        attention_kernel,
        grid_spec=pltpu.PrefetchScalarGridSpec(
            num_scalar_prefetch=1,
            grid=(pairs,),
            in_specs=[
                pl.BlockSpec((rows, qblock), lambda p, n: (0, p)),
                pl.BlockSpec((rows, lanes), lambda p, n: (0, kstart + p)),
                pl.BlockSpec((rows, lanes), lambda p, n: (0, vstart + p)),
                pl.BlockSpec((rows, lanes), lambda p, n: (0, 0)),
                pl.BlockSpec((rows, lanes), lambda p, n: (0, 0)),
                pl.BlockSpec((span, lanes), lambda p, n: (0, p)),
                pl.BlockSpec((span, lanes), lambda p, n: (0, p)),
            ],
            out_specs=pl.BlockSpec((rows, qblock), lambda p, n: (0, p)),
        ),
        out_shape=jax.ShapeDtypeStruct((rows, qwidth), jnp.bfloat16),
        interpret=interpret,
    )(length, mixed, mixed, mixed, cosine, sine, kc, vc)


def attend(tokens, qkv_weight, out_weight, norm_attn, keys_cache, values_cache, length, interpret=False):
    rows = tokens.shape[0]
    half = HEAD // 2
    normed = rms_scale(tokens, norm_attn).astype(jnp.bfloat16)
    mixed = jnp.dot(normed, qkv_weight, preferred_element_type=jnp.float32)
    places = (length + jnp.arange(rows, dtype=jnp.int32)).astype(jnp.float32)
    index = (jnp.arange(2 * HEAD, dtype=jnp.int32) % half).astype(jnp.float32)
    freq = 10000.0 ** (-index / half)
    angle = places[:, None] * freq[None, :]
    cosine = jnp.cos(angle)
    sine = jnp.sin(angle)
    heads_out = attention_core(
        length.reshape(1).astype(jnp.int32),
        mixed,
        cosine,
        sine,
        keys_cache,
        values_cache,
        interpret=interpret,
    )
    return jnp.dot(heads_out, out_weight, preferred_element_type=jnp.float32)


def swap(piece, bit):
    return lax.ppermute(piece, "q", [(i, i ^ bit) for i in range(lax.axis_size("q"))])


def on_device(
    tokens,
    qkv_weight,
    out_weight,
    norm_attn,
    norm_expert,
    keys_cache,
    values_cache,
    lengths,
    routes,
    gates,
    gate_up,
    down_weight,
):
    slices = lax.axis_size("q")
    width_dev = down_weight.shape[1]
    own_gu = gate_up[0]
    own_dw = down_weight[0]
    far_gu = swap(own_gu, 2)
    far_dw = swap(own_dw, 2)
    side_gu = swap(own_gu, 1)
    side_dw = swap(own_dw, 1)
    branch = attend(
        tokens, qkv_weight, out_weight, norm_attn, keys_cache[0], values_cache[0], lengths[0]
    )
    branch, far_gu, far_dw = lax.optimization_barrier((branch, far_gu, far_dw))
    gate_up_all = jnp.concatenate([own_gu, far_gu, side_gu, swap(far_gu, 1)], axis=1)
    down_all = jnp.concatenate([own_dw, far_dw, side_dw, swap(far_dw, 1)], axis=0)
    carried = tokens.astype(jnp.float32) + 0.22 * branch
    normed = rms_scale(carried, norm_expert).astype(jnp.bfloat16)
    rows, width = normed.shape
    part = width // 2
    capacity = CAPACITY
    hits = routes[:, :, None] == jnp.arange(EXPERTS, dtype=jnp.int32)[None, None, :]
    marks = jnp.any(hits, axis=1)
    weight = jnp.sum(jnp.where(hits, gates[:, :, None], 0.0), axis=1)
    lower = (
        jnp.arange(rows, dtype=jnp.int32)[:, None] > jnp.arange(rows, dtype=jnp.int32)[None, :]
    ).astype(jnp.bfloat16)
    before = jnp.dot(lower, marks.astype(jnp.bfloat16), preferred_element_type=jnp.float32)
    slot = before.astype(jnp.int32)
    pick = marks[:, :, None] & (
        slot[:, :, None] == jnp.arange(capacity, dtype=jnp.int32)[None, None, :]
    )
    empty = jnp.zeros_like(pick)
    pick_lo = jnp.concatenate([pick, empty], axis=2).astype(jnp.bfloat16)
    pick_hi = jnp.concatenate([empty, pick], axis=2).astype(jnp.bfloat16)
    outgoing = jnp.einsum(
        "ter,tw->erw", pick_lo, normed[:, :part], preferred_element_type=jnp.float32
    ) + jnp.einsum("ter,tw->erw", pick_hi, normed[:, part:], preferred_element_type=jnp.float32)
    received = lax.all_to_all(
        outgoing.astype(jnp.bfloat16), ("req", "h"), split_axis=0, concat_axis=0, tiled=True
    )
    joined = jnp.concatenate([received[:, :capacity], received[:, capacity:]], axis=2)
    pieces = gate_up_all.reshape(gate_up_all.shape[0], slices, 2 * width_dev)
    gate_cols = pieces[..., :width_dev].reshape(gate_up_all.shape[0], slices * width_dev)
    up_cols = pieces[..., width_dev:].reshape(gate_up_all.shape[0], slices * width_dev)
    both = jnp.einsum(
        "scw,wh->sch",
        joined,
        jnp.concatenate([gate_cols, up_cols], axis=1),
        preferred_element_type=jnp.float32,
    )
    inner = slices * width_dev
    hidden = (jax.nn.silu(both[..., :inner]) * both[..., inner:]).astype(jnp.bfloat16)
    produced = jnp.einsum(
        "sch,hw->scw", hidden, down_all, preferred_element_type=jnp.float32
    ).astype(jnp.bfloat16)
    back = jnp.concatenate([produced[..., :part], produced[..., part:]], axis=1)
    results = lax.all_to_all(back, ("req", "h"), split_axis=0, concat_axis=0, tiled=True)
    scale = jnp.where(pick, weight[:, :, None], 0.0)
    output = jnp.concatenate([results[:, :capacity], results[:, capacity:]], axis=2)
    mix = jnp.einsum(
        "tec,ecw->tw",
        scale,
        output.astype(jnp.float32),
        precision=lax.Precision.HIGHEST,
        preferred_element_type=jnp.float32,
    )
    return (branch.astype(jnp.bfloat16), mix.astype(jnp.bfloat16))


def solution(mesh):
    groups = mesh.shape["req"]
    slices = groups * mesh.shape["cuts"] // EXPERTS
    split = jax.sharding.Mesh(
        mesh.devices.reshape(groups, mesh.shape["cuts"] // slices, slices), ("req", "h", "q")
    )
    rows = ("req", "h", "q")
    placed = (
        P(rows, None),
        P(),
        P(),
        P(),
        P(),
        P(rows, None, None),
        P(rows, None, None),
        P(rows),
        P(rows, None),
        P(rows, None),
        P(rows, None, None),
        P(rows, None, None),
    )
    return jax.shard_map(
        on_device,
        mesh=split,
        in_specs=placed,
        out_specs=(P(rows, None), P(rows, None)),
        check_vma=False,
    )
```

```python
import jax
import jax.numpy as jnp
from jax import lax
from jax.sharding import PartitionSpec as P
from jax.experimental import pallas as pl
from jax.experimental.pallas import tpu as pltpu

HEADS = 16
KV_HEADS = 8
HEAD = 64
EXPERTS = 32
TOP = 8
CAPACITY = 40


def rms_scale(values, gain):
    wide = values.astype(jnp.float32)
    power = jnp.mean(wide * wide, axis=-1, keepdims=True)
    return wide * lax.rsqrt(power + 1e-06) * gain


def rotate(vectors, places):
    half = vectors.shape[-1] // 2
    freq = 10000.0 ** (-jnp.arange(half, dtype=jnp.float32) / half)
    angle = places[:, None] * freq[None, :]
    cosine = jnp.cos(angle)[:, None, :]
    sine = jnp.sin(angle)[:, None, :]
    first = vectors[..., :half]
    second = vectors[..., half:]
    return jnp.concatenate(
        [first * cosine - second * sine, second * cosine + first * sine], axis=-1
    )


def turn(values, cosine, sine, lead, half):
    partner = jnp.where(
        lead, pltpu.roll(values, values.shape[1] - half, 1), pltpu.roll(values, half, 1)
    )
    return jnp.where(lead, values * cosine - partner * sine, values * cosine + partner * sine)


def attention_kernel(length_ref, q_ref, k_ref, v_ref, cos_ref, sin_ref, kc_ref, vc_ref, o_ref):
    length = length_ref[0]
    span, lanes = kc_ref.shape
    rows = k_ref.shape[0]
    half = lanes // 2
    quarter = HEAD // 2
    cosine = cos_ref[...]
    sine = sin_ref[...]
    lane = lax.broadcasted_iota(jnp.int32, (rows, lanes), 1)
    lead = lane % HEAD < quarter
    low = lane < half
    kc = kc_ref[...]
    vc = vc_ref[...]
    kn = turn(k_ref[...], cosine, sine, lead, quarter).astype(jnp.bfloat16)
    vn = v_ref[...].astype(jnp.bfloat16)
    column = lax.broadcasted_iota(jnp.int32, (rows, span), 1)
    cache_ok = column < length
    new_col = lax.broadcasted_iota(jnp.int32, (rows, rows), 1)
    new_row = lax.broadcasted_iota(jnp.int32, (rows, rows), 0)
    new_ok = new_col <= new_row

    def scaled(values):
        rotated = turn(values, cosine, sine, lead, quarter).astype(jnp.bfloat16)
        return (rotated * 0.015625).astype(jnp.bfloat16).astype(jnp.float32)

    first = scaled(q_ref[:, :lanes])
    second = scaled(q_ref[:, lanes:])
    queries = (
        jnp.where(low, first, 0.0),
        jnp.where(low, pltpu.roll(first, half, 1), 0.0),
        jnp.where(low, 0.0, pltpu.roll(second, half, 1)),
        jnp.where(low, 0.0, second),
    )
    contract = (((1,), (1,)), ((), ()))
    outs = []
    for q in queries:
        q = q.astype(jnp.bfloat16)
        s = lax.dot_general(q, kc, contract, preferred_element_type=jnp.float32)
        s = jnp.where(cache_ok, s, -1e30)
        sn = lax.dot_general(q, kn, contract, preferred_element_type=jnp.float32)
        sn = jnp.where(new_ok, sn, -1e30)
        top = jnp.maximum(jnp.max(s, axis=1, keepdims=True), jnp.max(sn, axis=1, keepdims=True))
        e = jnp.exp(s - top)
        en = jnp.exp(sn - top)
        total = jnp.sum(e, axis=1, keepdims=True) + jnp.sum(en, axis=1, keepdims=True)
        inverse = 1.0 / total
        w = (e * inverse).astype(jnp.bfloat16)
        wn = (en * inverse).astype(jnp.bfloat16)
        o = jnp.dot(w, vc, preferred_element_type=jnp.float32) + jnp.dot(
            wn, vn, preferred_element_type=jnp.float32
        )
        outs.append(o.astype(jnp.bfloat16).astype(jnp.float32))
    left = jnp.where(low, outs[0], pltpu.roll(outs[1], half, 1))
    right = jnp.where(low, pltpu.roll(outs[2], half, 1), outs[3])
    o_ref[:, :lanes] = left.astype(jnp.bfloat16)
    o_ref[:, lanes:] = right.astype(jnp.bfloat16)


def attention_core(length, mixed, cosine, sine, kc, vc, interpret=False):
    rows = mixed.shape[0]
    span, kvwidth = kc.shape
    qwidth = HEADS * HEAD
    lanes = 2 * HEAD
    pairs = kvwidth // lanes
    qblock = qwidth // pairs
    kstart = qwidth // lanes
    vstart = kstart + pairs
    return pl.pallas_call(
        attention_kernel,
        grid_spec=pltpu.PrefetchScalarGridSpec(
            num_scalar_prefetch=1,
            grid=(pairs,),
            in_specs=[
                pl.BlockSpec((rows, qblock), lambda p, n: (0, p)),
                pl.BlockSpec((rows, lanes), lambda p, n: (0, kstart + p)),
                pl.BlockSpec((rows, lanes), lambda p, n: (0, vstart + p)),
                pl.BlockSpec((rows, lanes), lambda p, n: (0, 0)),
                pl.BlockSpec((rows, lanes), lambda p, n: (0, 0)),
                pl.BlockSpec((span, lanes), lambda p, n: (0, p)),
                pl.BlockSpec((span, lanes), lambda p, n: (0, p)),
            ],
            out_specs=pl.BlockSpec((rows, qblock), lambda p, n: (0, p)),
        ),
        out_shape=jax.ShapeDtypeStruct((rows, qwidth), jnp.bfloat16),
        interpret=interpret,
    )(length, mixed, mixed, mixed, cosine, sine, kc, vc)


def attend(tokens, qkv_weight, out_weight, norm_attn, keys_cache, values_cache, length, interpret=False):
    rows = tokens.shape[0]
    half = HEAD // 2
    normed = rms_scale(tokens, norm_attn).astype(jnp.bfloat16)
    mixed = jnp.dot(normed, qkv_weight, preferred_element_type=jnp.float32)
    places = (length + jnp.arange(rows, dtype=jnp.int32)).astype(jnp.float32)
    index = (jnp.arange(2 * HEAD, dtype=jnp.int32) % half).astype(jnp.float32)
    freq = 10000.0 ** (-index / half)
    angle = places[:, None] * freq[None, :]
    cosine = jnp.cos(angle)
    sine = jnp.sin(angle)
    heads_out = attention_core(
        length.reshape(1).astype(jnp.int32),
        mixed,
        cosine,
        sine,
        keys_cache,
        values_cache,
        interpret=interpret,
    )
    return jnp.dot(heads_out, out_weight, preferred_element_type=jnp.float32)


def swap(piece, bit):
    return lax.ppermute(piece, "q", [(i, i ^ bit) for i in range(lax.axis_size("q"))])


def on_device(
    tokens,
    qkv_weight,
    out_weight,
    norm_attn,
    norm_expert,
    keys_cache,
    values_cache,
    lengths,
    routes,
    gates,
    gate_up,
    down_weight,
):
    slices = lax.axis_size("q")
    width_dev = down_weight.shape[1]
    own_gu = gate_up[0]
    own_dw = down_weight[0]
    far_gu = swap(own_gu, 2)
    far_dw = swap(own_dw, 2)
    side_gu = swap(own_gu, 1)
    side_dw = swap(own_dw, 1)
    branch = attend(
        tokens, qkv_weight, out_weight, norm_attn, keys_cache[0], values_cache[0], lengths[0]
    )
    branch, far_gu, far_dw = lax.optimization_barrier((branch, far_gu, far_dw))
    gate_up_all = jnp.concatenate([own_gu, far_gu, side_gu, swap(far_gu, 1)], axis=1)
    down_all = jnp.concatenate([own_dw, far_dw, side_dw, swap(far_dw, 1)], axis=0)
    carried = tokens.astype(jnp.float32) + 0.22 * branch
    normed = rms_scale(carried, norm_expert).astype(jnp.bfloat16)
    rows, width = normed.shape
    part = width // 2
    capacity = CAPACITY
    hits = routes[:, :, None] == jnp.arange(EXPERTS, dtype=jnp.int32)[None, None, :]
    marks = jnp.any(hits, axis=1)
    weight = jnp.sum(jnp.where(hits, gates[:, :, None], 0.0), axis=1)
    lower = (
        jnp.arange(rows, dtype=jnp.int32)[:, None] > jnp.arange(rows, dtype=jnp.int32)[None, :]
    ).astype(jnp.bfloat16)
    before = jnp.dot(lower, marks.astype(jnp.bfloat16), preferred_element_type=jnp.float32)
    slot = before.astype(jnp.int32)
    pick = marks[:, :, None] & (
        slot[:, :, None] == jnp.arange(capacity, dtype=jnp.int32)[None, None, :]
    )
    empty = jnp.zeros_like(pick)
    pick_lo = jnp.concatenate([pick, empty], axis=2).astype(jnp.bfloat16)
    pick_hi = jnp.concatenate([empty, pick], axis=2).astype(jnp.bfloat16)
    outgoing = jnp.einsum(
        "ter,tw->erw",
        jnp.concatenate([pick_lo, pick_hi], axis=0),
        jnp.concatenate([normed[:, :part], normed[:, part:]], axis=0),
        preferred_element_type=jnp.float32,
    )
    received = lax.all_to_all(
        outgoing.astype(jnp.bfloat16), ("req", "h"), split_axis=0, concat_axis=0, tiled=True
    )
    joined = jnp.concatenate([received[:, :capacity], received[:, capacity:]], axis=2)
    pieces = gate_up_all.reshape(gate_up_all.shape[0], slices, 2 * width_dev)
    gate_cols = pieces[..., :width_dev].reshape(gate_up_all.shape[0], slices * width_dev)
    up_cols = pieces[..., width_dev:].reshape(gate_up_all.shape[0], slices * width_dev)
    both = jnp.einsum(
        "scw,wh->sch",
        joined,
        jnp.concatenate([gate_cols, up_cols], axis=1),
        preferred_element_type=jnp.float32,
    )
    inner = slices * width_dev
    hidden = (jax.nn.silu(both[..., :inner]) * both[..., inner:]).astype(jnp.bfloat16)
    produced = jnp.einsum(
        "sch,hw->scw", hidden, down_all, preferred_element_type=jnp.float32
    ).astype(jnp.bfloat16)
    back = jnp.concatenate([produced[..., :part], produced[..., part:]], axis=1)
    results = lax.all_to_all(back, ("req", "h"), split_axis=0, concat_axis=0, tiled=True)
    scale = jnp.where(pick, weight[:, :, None], 0.0)
    wide = results.astype(jnp.float32)
    halves = [
        jnp.einsum(
            "tec,ecw->tw",
            scale,
            piece,
            precision=lax.Precision.HIGHEST,
            preferred_element_type=jnp.float32,
        )
        for piece in (wide[:, :capacity], wide[:, capacity:])
    ]
    mix = jnp.concatenate(halves, axis=1)
    return (branch.astype(jnp.bfloat16), mix.astype(jnp.bfloat16))


def solution(mesh):
    groups = mesh.shape["req"]
    slices = groups * mesh.shape["cuts"] // EXPERTS
    split = jax.sharding.Mesh(
        mesh.devices.reshape(groups, mesh.shape["cuts"] // slices, slices), ("req", "h", "q")
    )
    rows = ("req", "h", "q")
    placed = (
        P(rows, None),
        P(),
        P(),
        P(),
        P(),
        P(rows, None, None),
        P(rows, None, None),
        P(rows),
        P(rows, None),
        P(rows, None),
        P(rows, None, None),
        P(rows, None, None),
    )
    return jax.shard_map(
        on_device,
        mesh=split,
        in_specs=placed,
        out_specs=(P(rows, None), P(rows, None)),
        check_vma=False,
    )
```

```python
import jax
import jax.numpy as jnp
from jax import lax
from jax.sharding import PartitionSpec as P
from jax.experimental import pallas as pl
from jax.experimental.pallas import tpu as pltpu

HEADS = 16
KV_HEADS = 8
HEAD = 64
EXPERTS = 32
TOP = 8
CAPACITY = 40


def rms_scale(values, gain):
    wide = values.astype(jnp.float32)
    power = jnp.mean(wide * wide, axis=-1, keepdims=True)
    return wide * lax.rsqrt(power + 1e-06) * gain


def rotate(vectors, places):
    half = vectors.shape[-1] // 2
    freq = 10000.0 ** (-jnp.arange(half, dtype=jnp.float32) / half)
    angle = places[:, None] * freq[None, :]
    cosine = jnp.cos(angle)[:, None, :]
    sine = jnp.sin(angle)[:, None, :]
    first = vectors[..., :half]
    second = vectors[..., half:]
    return jnp.concatenate(
        [first * cosine - second * sine, second * cosine + first * sine], axis=-1
    )


def turn(values, cosine, sine, lead, half):
    partner = jnp.where(
        lead, pltpu.roll(values, values.shape[1] - half, 1), pltpu.roll(values, half, 1)
    )
    return jnp.where(lead, values * cosine - partner * sine, values * cosine + partner * sine)


def attention_kernel(length_ref, q_ref, k_ref, v_ref, cos_ref, sin_ref, kc_ref, vc_ref, o_ref):
    length = length_ref[0]
    span, lanes = kc_ref.shape
    rows = k_ref.shape[0]
    half = lanes // 2
    quarter = HEAD // 2
    cosine = cos_ref[...]
    sine = sin_ref[...]
    lane = lax.broadcasted_iota(jnp.int32, (rows, lanes), 1)
    lead = lane % HEAD < quarter
    low = lane < half
    kc = kc_ref[...]
    vc = vc_ref[...]
    kn = turn(k_ref[...], cosine, sine, lead, quarter).astype(jnp.bfloat16)
    vn = v_ref[...].astype(jnp.bfloat16)
    column = lax.broadcasted_iota(jnp.int32, (rows, span), 1)
    cache_ok = column < length
    new_col = lax.broadcasted_iota(jnp.int32, (rows, rows), 1)
    new_row = lax.broadcasted_iota(jnp.int32, (rows, rows), 0)
    new_ok = new_col <= new_row

    def scaled(values):
        rotated = turn(values, cosine, sine, lead, quarter).astype(jnp.bfloat16)
        return (rotated * 0.015625).astype(jnp.bfloat16).astype(jnp.float32)

    first = scaled(q_ref[:, :lanes])
    second = scaled(q_ref[:, lanes:])
    queries = (
        jnp.where(low, first, 0.0),
        jnp.where(low, pltpu.roll(first, half, 1), 0.0),
        jnp.where(low, 0.0, pltpu.roll(second, half, 1)),
        jnp.where(low, 0.0, second),
    )
    contract = (((1,), (1,)), ((), ()))
    outs = []
    for q in queries:
        q = q.astype(jnp.bfloat16)
        s = lax.dot_general(q, kc, contract, preferred_element_type=jnp.float32)
        s = jnp.where(cache_ok, s, -1e30)
        sn = lax.dot_general(q, kn, contract, preferred_element_type=jnp.float32)
        sn = jnp.where(new_ok, sn, -1e30)
        top = jnp.maximum(jnp.max(s, axis=1, keepdims=True), jnp.max(sn, axis=1, keepdims=True))
        e = jnp.exp(s - top)
        en = jnp.exp(sn - top)
        total = jnp.sum(e, axis=1, keepdims=True) + jnp.sum(en, axis=1, keepdims=True)
        inverse = 1.0 / total
        w = (e * inverse).astype(jnp.bfloat16)
        wn = (en * inverse).astype(jnp.bfloat16)
        o = jnp.dot(w, vc, preferred_element_type=jnp.float32) + jnp.dot(
            wn, vn, preferred_element_type=jnp.float32
        )
        o = o.astype(jnp.bfloat16).astype(jnp.float32)
        j = len(outs)
        outs.append(j)
        place = slice(0, lanes) if j < 2 else slice(lanes, 2 * lanes)
        if j % 2 == 0:
            o_ref[:, place] = o.astype(jnp.bfloat16)
        else:
            kept = o_ref[:, place].astype(jnp.float32)
            if j == 1:
                merged = jnp.where(low, kept, pltpu.roll(o, half, 1))
            else:
                merged = jnp.where(low, pltpu.roll(kept, half, 1), o)
            o_ref[:, place] = merged.astype(jnp.bfloat16)


def attention_core(length, mixed, cosine, sine, kc, vc, interpret=False):
    rows = mixed.shape[0]
    span, kvwidth = kc.shape
    qwidth = HEADS * HEAD
    lanes = 2 * HEAD
    pairs = kvwidth // lanes
    qblock = qwidth // pairs
    kstart = qwidth // lanes
    vstart = kstart + pairs
    return pl.pallas_call(
        attention_kernel,
        grid_spec=pltpu.PrefetchScalarGridSpec(
            num_scalar_prefetch=1,
            grid=(pairs,),
            in_specs=[
                pl.BlockSpec((rows, qblock), lambda p, n: (0, p)),
                pl.BlockSpec((rows, lanes), lambda p, n: (0, kstart + p)),
                pl.BlockSpec((rows, lanes), lambda p, n: (0, vstart + p)),
                pl.BlockSpec((rows, lanes), lambda p, n: (0, 0)),
                pl.BlockSpec((rows, lanes), lambda p, n: (0, 0)),
                pl.BlockSpec((span, lanes), lambda p, n: (0, p)),
                pl.BlockSpec((span, lanes), lambda p, n: (0, p)),
            ],
            out_specs=pl.BlockSpec((rows, qblock), lambda p, n: (0, p)),
        ),
        out_shape=jax.ShapeDtypeStruct((rows, qwidth), jnp.bfloat16),
        interpret=interpret,
    )(length, mixed, mixed, mixed, cosine, sine, kc, vc)


def attend(tokens, qkv_weight, out_weight, norm_attn, keys_cache, values_cache, length, interpret=False):
    rows = tokens.shape[0]
    half = HEAD // 2
    normed = rms_scale(tokens, norm_attn).astype(jnp.bfloat16)
    mixed = jnp.dot(normed, qkv_weight, preferred_element_type=jnp.float32)
    places = (length + jnp.arange(rows, dtype=jnp.int32)).astype(jnp.float32)
    index = (jnp.arange(2 * HEAD, dtype=jnp.int32) % half).astype(jnp.float32)
    freq = 10000.0 ** (-index / half)
    angle = places[:, None] * freq[None, :]
    cosine = jnp.cos(angle)
    sine = jnp.sin(angle)
    heads_out = attention_core(
        length.reshape(1).astype(jnp.int32),
        mixed,
        cosine,
        sine,
        keys_cache,
        values_cache,
        interpret=interpret,
    )
    return jnp.dot(heads_out, out_weight, preferred_element_type=jnp.float32)


def swap(piece, bit):
    return lax.ppermute(piece, "q", [(i, i ^ bit) for i in range(lax.axis_size("q"))])


def on_device(
    tokens,
    qkv_weight,
    out_weight,
    norm_attn,
    norm_expert,
    keys_cache,
    values_cache,
    lengths,
    routes,
    gates,
    gate_up,
    down_weight,
):
    slices = lax.axis_size("q")
    width_dev = down_weight.shape[1]
    own_gu = gate_up[0]
    own_dw = down_weight[0]
    far_gu = swap(own_gu, 2)
    far_dw = swap(own_dw, 2)
    side_gu = swap(own_gu, 1)
    side_dw = swap(own_dw, 1)
    branch = attend(
        tokens, qkv_weight, out_weight, norm_attn, keys_cache[0], values_cache[0], lengths[0]
    )
    branch, far_gu, far_dw = lax.optimization_barrier((branch, far_gu, far_dw))
    gate_up_all = jnp.concatenate([own_gu, far_gu, side_gu, swap(far_gu, 1)], axis=1)
    down_all = jnp.concatenate([own_dw, far_dw, side_dw, swap(far_dw, 1)], axis=0)
    carried = tokens.astype(jnp.float32) + 0.22 * branch
    normed = rms_scale(carried, norm_expert).astype(jnp.bfloat16)
    rows, width = normed.shape
    part = width // 2
    capacity = CAPACITY
    hits = routes[:, :, None] == jnp.arange(EXPERTS, dtype=jnp.int32)[None, None, :]
    marks = jnp.any(hits, axis=1)
    weight = jnp.sum(jnp.where(hits, gates[:, :, None], 0.0), axis=1)
    lower = (
        jnp.arange(rows, dtype=jnp.int32)[:, None] > jnp.arange(rows, dtype=jnp.int32)[None, :]
    ).astype(jnp.bfloat16)
    before = jnp.dot(lower, marks.astype(jnp.bfloat16), preferred_element_type=jnp.float32)
    slot = before.astype(jnp.int32)
    pick = marks[:, :, None] & (
        slot[:, :, None] == jnp.arange(capacity, dtype=jnp.int32)[None, None, :]
    )
    empty = jnp.zeros_like(pick)
    pick_lo = jnp.concatenate([pick, empty], axis=2).astype(jnp.bfloat16)
    pick_hi = jnp.concatenate([empty, pick], axis=2).astype(jnp.bfloat16)
    outgoing = jnp.einsum(
        "ter,tw->erw",
        jnp.concatenate([pick_lo, pick_hi], axis=0),
        jnp.concatenate([normed[:, :part], normed[:, part:]], axis=0),
        preferred_element_type=jnp.float32,
    )
    received = lax.all_to_all(
        outgoing.astype(jnp.bfloat16), ("req", "h"), split_axis=0, concat_axis=0, tiled=True
    )
    joined = jnp.concatenate([received[:, :capacity], received[:, capacity:]], axis=2)
    pieces = gate_up_all.reshape(gate_up_all.shape[0], slices, 2 * width_dev)
    gate_cols = pieces[..., :width_dev].reshape(gate_up_all.shape[0], slices * width_dev)
    up_cols = pieces[..., width_dev:].reshape(gate_up_all.shape[0], slices * width_dev)
    both = jnp.einsum(
        "scw,wh->sch",
        joined,
        jnp.concatenate([gate_cols, up_cols], axis=1),
        preferred_element_type=jnp.float32,
    )
    inner = slices * width_dev
    hidden = (jax.nn.silu(both[..., :inner]) * both[..., inner:]).astype(jnp.bfloat16)
    produced = jnp.einsum(
        "sch,hw->scw", hidden, down_all, preferred_element_type=jnp.float32
    ).astype(jnp.bfloat16)
    back = jnp.concatenate([produced[..., :part], produced[..., part:]], axis=1)
    results = lax.all_to_all(back, ("req", "h"), split_axis=0, concat_axis=0, tiled=True)
    scale = jnp.where(pick, weight[:, :, None], 0.0)
    output = jnp.concatenate([results[:, :capacity], results[:, capacity:]], axis=2)
    mix = jnp.einsum(
        "tec,ecw->tw",
        scale,
        output.astype(jnp.float32),
        precision=lax.Precision.HIGHEST,
        preferred_element_type=jnp.float32,
    )
    return (branch.astype(jnp.bfloat16), mix.astype(jnp.bfloat16))


def solution(mesh):
    groups = mesh.shape["req"]
    slices = groups * mesh.shape["cuts"] // EXPERTS
    split = jax.sharding.Mesh(
        mesh.devices.reshape(groups, mesh.shape["cuts"] // slices, slices), ("req", "h", "q")
    )
    rows = ("req", "h", "q")
    placed = (
        P(rows, None),
        P(),
        P(),
        P(),
        P(),
        P(rows, None, None),
        P(rows, None, None),
        P(rows),
        P(rows, None),
        P(rows, None),
        P(rows, None, None),
        P(rows, None, None),
    )
    return jax.shard_map(
        on_device,
        mesh=split,
        in_specs=placed,
        out_specs=(P(rows, None), P(rows, None)),
        check_vma=False,
    )
```

```python
import jax
import jax.numpy as jnp
from jax import lax
from jax.sharding import PartitionSpec as P
from jax.experimental import pallas as pl
from jax.experimental.pallas import tpu as pltpu

HEADS = 16
KV_HEADS = 8
HEAD = 64
EXPERTS = 32
TOP = 8
CAPACITY = 40


def rms_scale(values, gain):
    wide = values.astype(jnp.float32)
    power = jnp.mean(wide * wide, axis=-1, keepdims=True)
    return wide * lax.rsqrt(power + 1e-06) * gain


def rotate(vectors, places):
    half = vectors.shape[-1] // 2
    freq = 10000.0 ** (-jnp.arange(half, dtype=jnp.float32) / half)
    angle = places[:, None] * freq[None, :]
    cosine = jnp.cos(angle)[:, None, :]
    sine = jnp.sin(angle)[:, None, :]
    first = vectors[..., :half]
    second = vectors[..., half:]
    return jnp.concatenate(
        [first * cosine - second * sine, second * cosine + first * sine], axis=-1
    )


def turn(values, cosine, sine, lead, half):
    partner = jnp.where(
        lead, pltpu.roll(values, values.shape[1] - half, 1), pltpu.roll(values, half, 1)
    )
    return jnp.where(lead, values * cosine - partner * sine, values * cosine + partner * sine)


def attention_kernel(
    length_ref, q_ref, k_ref, v_ref, cos_ref, sin_ref, kc_ref, vc_ref, o_ref, s_ref, sn_ref, w_ref, wn_ref
):
    length = length_ref[0]
    span, lanes = kc_ref.shape
    rows = k_ref.shape[0]
    half = lanes // 2
    quarter = HEAD // 2
    cosine = cos_ref[...]
    sine = sin_ref[...]
    lane = lax.broadcasted_iota(jnp.int32, (rows, lanes), 1)
    lead = lane % HEAD < quarter
    low = lane < half
    kc = kc_ref[...]
    vc = vc_ref[...]
    kn = turn(k_ref[...], cosine, sine, lead, quarter).astype(jnp.bfloat16)
    vn = v_ref[...].astype(jnp.bfloat16)
    def scaled(values):
        rotated = turn(values, cosine, sine, lead, quarter).astype(jnp.bfloat16)
        return (rotated * 0.015625).astype(jnp.bfloat16).astype(jnp.float32)

    first = scaled(q_ref[:, :lanes])
    second = scaled(q_ref[:, lanes:])
    queries = (
        jnp.where(low, first, 0.0),
        jnp.where(low, pltpu.roll(first, half, 1), 0.0),
        jnp.where(low, 0.0, pltpu.roll(second, half, 1)),
        jnp.where(low, 0.0, second),
    )
    contract = (((1,), (1,)), ((), ()))
    chunk = 32
    outs = []
    for q in queries:
        q = q.astype(jnp.bfloat16)
        s_ref[...] = lax.dot_general(q, kc, contract, preferred_element_type=jnp.float32)
        sn_ref[...] = lax.dot_general(q, kn, contract, preferred_element_type=jnp.float32)
        for i in range(rows // chunk):
            at = slice(i * chunk, (i + 1) * chunk)
            column = lax.broadcasted_iota(jnp.int32, (chunk, span), 1)
            s = jnp.where(column < length, s_ref[at, :], -1e30)
            new_col = lax.broadcasted_iota(jnp.int32, (chunk, rows), 1)
            new_row = lax.broadcasted_iota(jnp.int32, (chunk, rows), 0) + i * chunk
            sn = jnp.where(new_col <= new_row, sn_ref[at, :], -1e30)
            top = jnp.maximum(
                jnp.max(s, axis=1, keepdims=True), jnp.max(sn, axis=1, keepdims=True)
            )
            e = jnp.exp(s - top)
            en = jnp.exp(sn - top)
            total = jnp.sum(e, axis=1, keepdims=True) + jnp.sum(en, axis=1, keepdims=True)
            inverse = 1.0 / total
            w_ref[at, :] = (e * inverse).astype(jnp.bfloat16)
            wn_ref[at, :] = (en * inverse).astype(jnp.bfloat16)
        o = jnp.dot(w_ref[...], vc, preferred_element_type=jnp.float32) + jnp.dot(
            wn_ref[...], vn, preferred_element_type=jnp.float32
        )
        o = o.astype(jnp.bfloat16).astype(jnp.float32)
        j = len(outs)
        outs.append(j)
        place = slice(0, lanes) if j < 2 else slice(lanes, 2 * lanes)
        if j % 2 == 0:
            o_ref[:, place] = o.astype(jnp.bfloat16)
        else:
            kept = o_ref[:, place].astype(jnp.float32)
            if j == 1:
                merged = jnp.where(low, kept, pltpu.roll(o, half, 1))
            else:
                merged = jnp.where(low, pltpu.roll(kept, half, 1), o)
            o_ref[:, place] = merged.astype(jnp.bfloat16)


def attention_core(length, mixed, cosine, sine, kc, vc, interpret=False):
    rows = mixed.shape[0]
    span, kvwidth = kc.shape
    qwidth = HEADS * HEAD
    lanes = 2 * HEAD
    pairs = kvwidth // lanes
    qblock = qwidth // pairs
    kstart = qwidth // lanes
    vstart = kstart + pairs
    return pl.pallas_call(
        attention_kernel,
        grid_spec=pltpu.PrefetchScalarGridSpec(
            num_scalar_prefetch=1,
            grid=(pairs,),
            in_specs=[
                pl.BlockSpec((rows, qblock), lambda p, n: (0, p)),
                pl.BlockSpec((rows, lanes), lambda p, n: (0, kstart + p)),
                pl.BlockSpec((rows, lanes), lambda p, n: (0, vstart + p)),
                pl.BlockSpec((rows, lanes), lambda p, n: (0, 0)),
                pl.BlockSpec((rows, lanes), lambda p, n: (0, 0)),
                pl.BlockSpec((span, lanes), lambda p, n: (0, p)),
                pl.BlockSpec((span, lanes), lambda p, n: (0, p)),
            ],
            out_specs=pl.BlockSpec((rows, qblock), lambda p, n: (0, p)),
            scratch_shapes=[
                pltpu.VMEM((rows, span), jnp.float32),
                pltpu.VMEM((rows, rows), jnp.float32),
                pltpu.VMEM((rows, span), jnp.bfloat16),
                pltpu.VMEM((rows, rows), jnp.bfloat16),
            ],
        ),
        out_shape=jax.ShapeDtypeStruct((rows, qwidth), jnp.bfloat16),
        interpret=interpret,
    )(length, mixed, mixed, mixed, cosine, sine, kc, vc)


def attend(tokens, qkv_weight, out_weight, norm_attn, keys_cache, values_cache, length, interpret=False):
    rows = tokens.shape[0]
    half = HEAD // 2
    normed = rms_scale(tokens, norm_attn).astype(jnp.bfloat16)
    mixed = jnp.dot(normed, qkv_weight, preferred_element_type=jnp.float32)
    places = (length + jnp.arange(rows, dtype=jnp.int32)).astype(jnp.float32)
    index = (jnp.arange(2 * HEAD, dtype=jnp.int32) % half).astype(jnp.float32)
    freq = 10000.0 ** (-index / half)
    angle = places[:, None] * freq[None, :]
    cosine = jnp.cos(angle)
    sine = jnp.sin(angle)
    heads_out = attention_core(
        length.reshape(1).astype(jnp.int32),
        mixed,
        cosine,
        sine,
        keys_cache,
        values_cache,
        interpret=interpret,
    )
    return jnp.dot(heads_out, out_weight, preferred_element_type=jnp.float32)


def swap(piece, bit):
    return lax.ppermute(piece, "q", [(i, i ^ bit) for i in range(lax.axis_size("q"))])


def on_device(
    tokens,
    qkv_weight,
    out_weight,
    norm_attn,
    norm_expert,
    keys_cache,
    values_cache,
    lengths,
    routes,
    gates,
    gate_up,
    down_weight,
):
    slices = lax.axis_size("q")
    width_dev = down_weight.shape[1]
    own_gu = gate_up[0]
    own_dw = down_weight[0]
    far_gu = swap(own_gu, 2)
    far_dw = swap(own_dw, 2)
    side_gu = swap(own_gu, 1)
    side_dw = swap(own_dw, 1)
    branch = attend(
        tokens, qkv_weight, out_weight, norm_attn, keys_cache[0], values_cache[0], lengths[0]
    )
    branch, far_gu, far_dw = lax.optimization_barrier((branch, far_gu, far_dw))
    gate_up_all = jnp.concatenate([own_gu, far_gu, side_gu, swap(far_gu, 1)], axis=1)
    down_all = jnp.concatenate([own_dw, far_dw, side_dw, swap(far_dw, 1)], axis=0)
    carried = tokens.astype(jnp.float32) + 0.22 * branch
    normed = rms_scale(carried, norm_expert).astype(jnp.bfloat16)
    rows, width = normed.shape
    part = width // 2
    capacity = CAPACITY
    hits = routes[:, :, None] == jnp.arange(EXPERTS, dtype=jnp.int32)[None, None, :]
    marks = jnp.any(hits, axis=1)
    weight = jnp.sum(jnp.where(hits, gates[:, :, None], 0.0), axis=1)
    lower = (
        jnp.arange(rows, dtype=jnp.int32)[:, None] > jnp.arange(rows, dtype=jnp.int32)[None, :]
    ).astype(jnp.bfloat16)
    before = jnp.dot(lower, marks.astype(jnp.bfloat16), preferred_element_type=jnp.float32)
    slot = before.astype(jnp.int32)
    pick = marks[:, :, None] & (
        slot[:, :, None] == jnp.arange(capacity, dtype=jnp.int32)[None, None, :]
    )
    empty = jnp.zeros_like(pick)
    pick_lo = jnp.concatenate([pick, empty], axis=2).astype(jnp.bfloat16)
    pick_hi = jnp.concatenate([empty, pick], axis=2).astype(jnp.bfloat16)
    outgoing = jnp.einsum(
        "ter,tw->erw",
        jnp.concatenate([pick_lo, pick_hi], axis=0),
        jnp.concatenate([normed[:, :part], normed[:, part:]], axis=0),
        preferred_element_type=jnp.float32,
    )
    received = lax.all_to_all(
        outgoing.astype(jnp.bfloat16), ("req", "h"), split_axis=0, concat_axis=0, tiled=True
    )
    joined = jnp.concatenate([received[:, :capacity], received[:, capacity:]], axis=2)
    pieces = gate_up_all.reshape(gate_up_all.shape[0], slices, 2 * width_dev)
    gate_cols = pieces[..., :width_dev].reshape(gate_up_all.shape[0], slices * width_dev)
    up_cols = pieces[..., width_dev:].reshape(gate_up_all.shape[0], slices * width_dev)
    both = jnp.einsum(
        "scw,wh->sch",
        joined,
        jnp.concatenate([gate_cols, up_cols], axis=1),
        preferred_element_type=jnp.float32,
    )
    inner = slices * width_dev
    hidden = (jax.nn.silu(both[..., :inner]) * both[..., inner:]).astype(jnp.bfloat16)
    produced = jnp.einsum(
        "sch,hw->scw", hidden, down_all, preferred_element_type=jnp.float32
    ).astype(jnp.bfloat16)
    back = jnp.concatenate([produced[..., :part], produced[..., part:]], axis=1)
    results = lax.all_to_all(back, ("req", "h"), split_axis=0, concat_axis=0, tiled=True)
    scale = jnp.where(pick, weight[:, :, None], 0.0)
    output = jnp.concatenate([results[:, :capacity], results[:, capacity:]], axis=2)
    mix = jnp.einsum(
        "tec,ecw->tw",
        scale,
        output.astype(jnp.float32),
        precision=lax.Precision.HIGHEST,
        preferred_element_type=jnp.float32,
    )
    return (branch.astype(jnp.bfloat16), mix.astype(jnp.bfloat16))


def solution(mesh):
    groups = mesh.shape["req"]
    slices = groups * mesh.shape["cuts"] // EXPERTS
    split = jax.sharding.Mesh(
        mesh.devices.reshape(groups, mesh.shape["cuts"] // slices, slices), ("req", "h", "q")
    )
    rows = ("req", "h", "q")
    placed = (
        P(rows, None),
        P(),
        P(),
        P(),
        P(),
        P(rows, None, None),
        P(rows, None, None),
        P(rows),
        P(rows, None),
        P(rows, None),
        P(rows, None, None),
        P(rows, None, None),
    )
    return jax.shard_map(
        on_device,
        mesh=split,
        in_specs=placed,
        out_specs=(P(rows, None), P(rows, None)),
        check_vma=False,
    )
```

```python
import jax
import jax.numpy as jnp
from jax import lax
from jax.sharding import PartitionSpec as P
from jax.experimental import pallas as pl
from jax.experimental.pallas import tpu as pltpu

HEADS = 16
KV_HEADS = 8
HEAD = 64
EXPERTS = 32
TOP = 8
CAPACITY = 40


def rms_scale(values, gain):
    wide = values.astype(jnp.float32)
    power = jnp.mean(wide * wide, axis=-1, keepdims=True)
    return wide * lax.rsqrt(power + 1e-06) * gain


def rotate(vectors, places):
    half = vectors.shape[-1] // 2
    freq = 10000.0 ** (-jnp.arange(half, dtype=jnp.float32) / half)
    angle = places[:, None] * freq[None, :]
    cosine = jnp.cos(angle)[:, None, :]
    sine = jnp.sin(angle)[:, None, :]
    first = vectors[..., :half]
    second = vectors[..., half:]
    return jnp.concatenate(
        [first * cosine - second * sine, second * cosine + first * sine], axis=-1
    )


def turn(values, cosine, sine, lead, half):
    partner = jnp.where(
        lead, pltpu.roll(values, values.shape[1] - half, 1), pltpu.roll(values, half, 1)
    )
    return jnp.where(lead, values * cosine - partner * sine, values * cosine + partner * sine)


def attention_kernel(length_ref, q_ref, k_ref, v_ref, cos_ref, sin_ref, kc_ref, vc_ref, o_ref):
    length = length_ref[0]
    span, lanes = kc_ref.shape
    rows = k_ref.shape[0]
    half = lanes // 2
    quarter = HEAD // 2
    cosine = cos_ref[...]
    sine = sin_ref[...]
    lane = lax.broadcasted_iota(jnp.int32, (rows, lanes), 1)
    lead = lane % HEAD < quarter
    low = lane < half
    kc = kc_ref[...]
    vc = vc_ref[...]
    kn = turn(k_ref[...], cosine, sine, lead, quarter).astype(jnp.bfloat16)
    vn = v_ref[...].astype(jnp.bfloat16)
    column = lax.broadcasted_iota(jnp.int32, (rows, span), 1)
    cache_ok = column < length
    new_col = lax.broadcasted_iota(jnp.int32, (rows, rows), 1)
    new_row = lax.broadcasted_iota(jnp.int32, (rows, rows), 0)
    new_ok = new_col <= new_row

    def scaled(values):
        rotated = turn(values, cosine, sine, lead, quarter).astype(jnp.bfloat16)
        return (rotated * 0.015625).astype(jnp.bfloat16).astype(jnp.float32)

    first = scaled(q_ref[:, :lanes])
    second = scaled(q_ref[:, lanes:])
    queries = (
        jnp.where(low, first, 0.0),
        jnp.where(low, pltpu.roll(first, half, 1), 0.0),
        jnp.where(low, 0.0, pltpu.roll(second, half, 1)),
        jnp.where(low, 0.0, second),
    )
    contract = (((1,), (1,)), ((), ()))
    outs = []
    for q in queries:
        q = q.astype(jnp.bfloat16)
        s = lax.dot_general(q, kc, contract, preferred_element_type=jnp.float32)
        s = jnp.where(cache_ok, s, -1e30)
        sn = lax.dot_general(q, kn, contract, preferred_element_type=jnp.float32)
        sn = jnp.where(new_ok, sn, -1e30)
        top = jnp.maximum(jnp.max(s, axis=1, keepdims=True), jnp.max(sn, axis=1, keepdims=True))
        e = jnp.exp(s - top)
        en = jnp.exp(sn - top)
        total = jnp.sum(e, axis=1, keepdims=True) + jnp.sum(en, axis=1, keepdims=True)
        inverse = 1.0 / total
        w = (e * inverse).astype(jnp.bfloat16)
        wn = (en * inverse).astype(jnp.bfloat16)
        o = jnp.dot(w, vc, preferred_element_type=jnp.float32) + jnp.dot(
            wn, vn, preferred_element_type=jnp.float32
        )
        o = o.astype(jnp.bfloat16).astype(jnp.float32)
        j = len(outs)
        outs.append(j)
        place = slice(0, lanes) if j < 2 else slice(lanes, 2 * lanes)
        if j % 2 == 0:
            o_ref[:, place] = o.astype(jnp.bfloat16)
        else:
            kept = o_ref[:, place].astype(jnp.float32)
            if j == 1:
                merged = jnp.where(low, kept, pltpu.roll(o, half, 1))
            else:
                merged = jnp.where(low, pltpu.roll(kept, half, 1), o)
            o_ref[:, place] = merged.astype(jnp.bfloat16)


def attention_core(length, mixed, cosine, sine, kc, vc, interpret=False):
    rows = mixed.shape[0]
    span, kvwidth = kc.shape
    qwidth = HEADS * HEAD
    lanes = 2 * HEAD
    pairs = kvwidth // lanes
    qblock = qwidth // pairs
    kstart = qwidth // lanes
    vstart = kstart + pairs
    return pl.pallas_call(
        attention_kernel,
        grid_spec=pltpu.PrefetchScalarGridSpec(
            num_scalar_prefetch=1,
            grid=(pairs,),
            in_specs=[
                pl.BlockSpec((rows, qblock), lambda p, n: (0, p)),
                pl.BlockSpec((rows, lanes), lambda p, n: (0, kstart + p)),
                pl.BlockSpec((rows, lanes), lambda p, n: (0, vstart + p)),
                pl.BlockSpec((rows, lanes), lambda p, n: (0, 0)),
                pl.BlockSpec((rows, lanes), lambda p, n: (0, 0)),
                pl.BlockSpec((span, lanes), lambda p, n: (0, p)),
                pl.BlockSpec((span, lanes), lambda p, n: (0, p)),
            ],
            out_specs=pl.BlockSpec((rows, qblock), lambda p, n: (0, p)),
        ),
        out_shape=jax.ShapeDtypeStruct((rows, qwidth), jnp.bfloat16),
        interpret=interpret,
    )(length, mixed, mixed, mixed, cosine, sine, kc, vc)


def attend(tokens, qkv_weight, out_weight, norm_attn, keys_cache, values_cache, length, interpret=False):
    rows = tokens.shape[0]
    half = HEAD // 2
    normed = rms_scale(tokens, norm_attn).astype(jnp.bfloat16)
    mixed = jnp.dot(normed, qkv_weight, preferred_element_type=jnp.float32)
    places = (length + jnp.arange(rows, dtype=jnp.int32)).astype(jnp.float32)
    index = (jnp.arange(2 * HEAD, dtype=jnp.int32) % half).astype(jnp.float32)
    freq = 10000.0 ** (-index / half)
    angle = places[:, None] * freq[None, :]
    cosine = jnp.cos(angle)
    sine = jnp.sin(angle)
    heads_out = attention_core(
        length.reshape(1).astype(jnp.int32),
        mixed,
        cosine,
        sine,
        keys_cache,
        values_cache,
        interpret=interpret,
    )
    return jnp.dot(heads_out, out_weight, preferred_element_type=jnp.float32)


def swap(piece, bit):
    return lax.ppermute(piece, "q", [(i, i ^ bit) for i in range(lax.axis_size("q"))])


def on_device(
    tokens,
    qkv_weight,
    out_weight,
    norm_attn,
    norm_expert,
    keys_cache,
    values_cache,
    lengths,
    routes,
    gates,
    gate_up,
    down_weight,
):
    slices = lax.axis_size("q")
    width_dev = down_weight.shape[1]
    own_gu = gate_up[0]
    own_dw = down_weight[0]
    far_gu = swap(own_gu, 2)
    far_dw = swap(own_dw, 2)
    side_gu = swap(own_gu, 1)
    side_dw = swap(own_dw, 1)
    branch = attend(
        tokens, qkv_weight, out_weight, norm_attn, keys_cache[0], values_cache[0], lengths[0]
    )
    branch, far_gu, far_dw = lax.optimization_barrier((branch, far_gu, far_dw))
    gate_up_all = jnp.concatenate([own_gu, far_gu, side_gu, swap(far_gu, 1)], axis=1)
    down_all = jnp.concatenate([own_dw, far_dw, side_dw, swap(far_dw, 1)], axis=0)
    carried = tokens.astype(jnp.float32) + 0.22 * branch
    normed = rms_scale(carried, norm_expert).astype(jnp.bfloat16)
    rows, width = normed.shape
    part = width // 2
    capacity = CAPACITY
    hits = routes[:, :, None] == jnp.arange(EXPERTS, dtype=jnp.int32)[None, None, :]
    marks = jnp.any(hits, axis=1)
    weight = jnp.sum(jnp.where(hits, gates[:, :, None], 0.0), axis=1)
    lower = (
        jnp.arange(rows, dtype=jnp.int32)[:, None] > jnp.arange(rows, dtype=jnp.int32)[None, :]
    ).astype(jnp.bfloat16)
    before = jnp.dot(lower, marks.astype(jnp.bfloat16), preferred_element_type=jnp.float32)
    slot = before.astype(jnp.int32)
    pick = marks[:, :, None] & (
        slot[:, :, None] == jnp.arange(capacity, dtype=jnp.int32)[None, None, :]
    )
    empty = jnp.zeros_like(pick)
    pick_lo = jnp.concatenate([pick, empty], axis=2).astype(jnp.bfloat16)
    pick_hi = jnp.concatenate([empty, pick], axis=2).astype(jnp.bfloat16)
    outgoing = jnp.einsum(
        "ter,tw->erw",
        jnp.concatenate([pick_lo, pick_hi], axis=0),
        jnp.concatenate([normed[:, :part], normed[:, part:]], axis=0),
        preferred_element_type=jnp.float32,
    )
    received = lax.all_to_all(
        outgoing.astype(jnp.bfloat16), ("req", "h"), split_axis=0, concat_axis=0, tiled=True
    )
    joined = jnp.concatenate([received[:, :capacity], received[:, capacity:]], axis=2)
    pieces = gate_up_all.reshape(gate_up_all.shape[0], slices, 2 * width_dev)
    gate_cols = pieces[..., :width_dev].reshape(gate_up_all.shape[0], slices * width_dev)
    up_cols = pieces[..., width_dev:].reshape(gate_up_all.shape[0], slices * width_dev)
    both = jnp.einsum(
        "scw,wh->sch",
        joined,
        jnp.concatenate([gate_cols, up_cols], axis=1),
        preferred_element_type=jnp.float32,
    )
    inner = slices * width_dev
    hidden = (jax.nn.silu(both[..., :inner]) * both[..., inner:]).astype(jnp.bfloat16)
    produced = jnp.einsum(
        "sch,hw->scw", hidden, down_all, preferred_element_type=jnp.float32
    ).astype(jnp.bfloat16)
    results = lax.all_to_all(produced, ("req", "h"), split_axis=0, concat_axis=0, tiled=True)
    scale = jnp.where(pick, weight[:, :, None], 0.0)
    mix = jnp.einsum(
        "tec,ecw->tw",
        scale,
        results.astype(jnp.float32),
        precision=lax.Precision.HIGHEST,
        preferred_element_type=jnp.float32,
    )
    return (branch.astype(jnp.bfloat16), mix.astype(jnp.bfloat16))


def solution(mesh):
    groups = mesh.shape["req"]
    slices = groups * mesh.shape["cuts"] // EXPERTS
    split = jax.sharding.Mesh(
        mesh.devices.reshape(groups, mesh.shape["cuts"] // slices, slices), ("req", "h", "q")
    )
    rows = ("req", "h", "q")
    placed = (
        P(rows, None),
        P(),
        P(),
        P(),
        P(),
        P(rows, None, None),
        P(rows, None, None),
        P(rows),
        P(rows, None),
        P(rows, None),
        P(rows, None, None),
        P(rows, None, None),
    )
    return jax.shard_map(
        on_device,
        mesh=split,
        in_specs=placed,
        out_specs=(P(rows, None), P(rows, None)),
        check_vma=False,
    )
```

```python
import jax
import jax.numpy as jnp
from jax import lax
from jax.sharding import PartitionSpec as P
from jax.experimental import pallas as pl
from jax.experimental.pallas import tpu as pltpu

HEADS = 16
KV_HEADS = 8
HEAD = 64
EXPERTS = 32
TOP = 8
CAPACITY = 40


def rms_scale(values, gain):
    wide = values.astype(jnp.float32)
    power = jnp.mean(wide * wide, axis=-1, keepdims=True)
    return wide * lax.rsqrt(power + 1e-06) * gain


def rotate(vectors, places):
    half = vectors.shape[-1] // 2
    freq = 10000.0 ** (-jnp.arange(half, dtype=jnp.float32) / half)
    angle = places[:, None] * freq[None, :]
    cosine = jnp.cos(angle)[:, None, :]
    sine = jnp.sin(angle)[:, None, :]
    first = vectors[..., :half]
    second = vectors[..., half:]
    return jnp.concatenate(
        [first * cosine - second * sine, second * cosine + first * sine], axis=-1
    )


def turn(values, cosine, sine, lead, half):
    partner = jnp.where(
        lead, pltpu.roll(values, values.shape[1] - half, 1), pltpu.roll(values, half, 1)
    )
    return jnp.where(lead, values * cosine - partner * sine, values * cosine + partner * sine)


def attention_kernel(length_ref, q_ref, k_ref, v_ref, cos_ref, sin_ref, kc_ref, vc_ref, o_ref):
    length = length_ref[0]
    span, lanes = kc_ref.shape
    rows = k_ref.shape[0]
    half = lanes // 2
    quarter = HEAD // 2
    cosine = cos_ref[...]
    sine = sin_ref[...]
    lane = lax.broadcasted_iota(jnp.int32, (rows, lanes), 1)
    lead = lane % HEAD < quarter
    low = lane < half
    kc = kc_ref[...]
    vc = vc_ref[...]
    kn = turn(k_ref[...], cosine, sine, lead, quarter).astype(jnp.bfloat16)
    vn = v_ref[...].astype(jnp.bfloat16)
    column = lax.broadcasted_iota(jnp.int32, (rows, span), 1)
    cache_ok = column < length
    new_col = lax.broadcasted_iota(jnp.int32, (rows, rows), 1)
    new_row = lax.broadcasted_iota(jnp.int32, (rows, rows), 0)
    new_ok = new_col <= new_row

    def scaled(values):
        rotated = turn(values, cosine, sine, lead, quarter).astype(jnp.bfloat16)
        return (rotated * 0.015625).astype(jnp.bfloat16).astype(jnp.float32)

    first = scaled(q_ref[:, :lanes])
    second = scaled(q_ref[:, lanes:])
    queries = (
        jnp.where(low, first, 0.0),
        jnp.where(low, pltpu.roll(first, half, 1), 0.0),
        jnp.where(low, 0.0, pltpu.roll(second, half, 1)),
        jnp.where(low, 0.0, second),
    )
    contract = (((1,), (1,)), ((), ()))
    outs = []
    for q in queries:
        q = q.astype(jnp.bfloat16)
        s = lax.dot_general(q, kc, contract, preferred_element_type=jnp.float32)
        s = jnp.where(cache_ok, s, -1e30)
        sn = lax.dot_general(q, kn, contract, preferred_element_type=jnp.float32)
        sn = jnp.where(new_ok, sn, -1e30)
        top = jnp.maximum(jnp.max(s, axis=1, keepdims=True), jnp.max(sn, axis=1, keepdims=True))
        e = jnp.exp(s - top)
        en = jnp.exp(sn - top)
        total = jnp.sum(e, axis=1, keepdims=True) + jnp.sum(en, axis=1, keepdims=True)
        inverse = 1.0 / total
        w = (e * inverse).astype(jnp.bfloat16)
        wn = (en * inverse).astype(jnp.bfloat16)
        o = jnp.dot(w, vc, preferred_element_type=jnp.float32) + jnp.dot(
            wn, vn, preferred_element_type=jnp.float32
        )
        o = o.astype(jnp.bfloat16).astype(jnp.float32)
        j = len(outs)
        outs.append(j)
        place = slice(0, lanes) if j < 2 else slice(lanes, 2 * lanes)
        if j % 2 == 0:
            o_ref[:, place] = o.astype(jnp.bfloat16)
        else:
            kept = o_ref[:, place].astype(jnp.float32)
            if j == 1:
                merged = jnp.where(low, kept, pltpu.roll(o, half, 1))
            else:
                merged = jnp.where(low, pltpu.roll(kept, half, 1), o)
            o_ref[:, place] = merged.astype(jnp.bfloat16)


def attention_core(length, mixed, cosine, sine, kc, vc, interpret=False):
    rows = mixed.shape[0]
    span, kvwidth = kc.shape
    qwidth = HEADS * HEAD
    lanes = 2 * HEAD
    pairs = kvwidth // lanes
    qblock = qwidth // pairs
    kstart = qwidth // lanes
    vstart = kstart + pairs
    return pl.pallas_call(
        attention_kernel,
        grid_spec=pltpu.PrefetchScalarGridSpec(
            num_scalar_prefetch=1,
            grid=(pairs,),
            in_specs=[
                pl.BlockSpec((rows, qblock), lambda p, n: (0, p)),
                pl.BlockSpec((rows, lanes), lambda p, n: (0, kstart + p)),
                pl.BlockSpec((rows, lanes), lambda p, n: (0, vstart + p)),
                pl.BlockSpec((rows, lanes), lambda p, n: (0, 0)),
                pl.BlockSpec((rows, lanes), lambda p, n: (0, 0)),
                pl.BlockSpec((span, lanes), lambda p, n: (0, p)),
                pl.BlockSpec((span, lanes), lambda p, n: (0, p)),
            ],
            out_specs=pl.BlockSpec((rows, qblock), lambda p, n: (0, p)),
        ),
        out_shape=jax.ShapeDtypeStruct((rows, qwidth), jnp.bfloat16),
        interpret=interpret,
    )(length, mixed, mixed, mixed, cosine, sine, kc, vc)


def attend(tokens, qkv_weight, out_weight, norm_attn, keys_cache, values_cache, length, interpret=False):
    rows = tokens.shape[0]
    half = HEAD // 2
    normed = rms_scale(tokens, norm_attn).astype(jnp.bfloat16)
    mixed = jnp.dot(normed, qkv_weight, preferred_element_type=jnp.float32)
    places = (length + jnp.arange(rows, dtype=jnp.int32)).astype(jnp.float32)
    index = (jnp.arange(2 * HEAD, dtype=jnp.int32) % half).astype(jnp.float32)
    freq = 10000.0 ** (-index / half)
    angle = places[:, None] * freq[None, :]
    cosine = jnp.cos(angle)
    sine = jnp.sin(angle)
    heads_out = attention_core(
        length.reshape(1).astype(jnp.int32),
        mixed,
        cosine,
        sine,
        keys_cache,
        values_cache,
        interpret=interpret,
    )
    return jnp.dot(heads_out, out_weight, preferred_element_type=jnp.float32)


def swap(piece, bit):
    return lax.ppermute(piece, "q", [(i, i ^ bit) for i in range(lax.axis_size("q"))])


def on_device(
    tokens,
    qkv_weight,
    out_weight,
    norm_attn,
    norm_expert,
    keys_cache,
    values_cache,
    lengths,
    routes,
    gates,
    gate_up,
    down_weight,
):
    slices = lax.axis_size("q")
    width_dev = down_weight.shape[1]
    own_gu = gate_up[0]
    own_dw = down_weight[0]
    far_gu = swap(own_gu, 2)
    far_dw = swap(own_dw, 2)
    side_gu = swap(own_gu, 1)
    side_dw = swap(own_dw, 1)
    branch = attend(
        tokens, qkv_weight, out_weight, norm_attn, keys_cache[0], values_cache[0], lengths[0]
    )
    branch, far_gu, far_dw = lax.optimization_barrier((branch, far_gu, far_dw))
    gate_up_all = jnp.concatenate([own_gu, far_gu, side_gu, swap(far_gu, 1)], axis=1)
    down_all = jnp.concatenate([own_dw, far_dw, side_dw, swap(far_dw, 1)], axis=0)
    carried = tokens.astype(jnp.float32) + 0.22 * branch
    normed = rms_scale(carried, norm_expert).astype(jnp.bfloat16)
    rows, width = normed.shape
    capacity = CAPACITY
    hits = routes[:, :, None] == jnp.arange(EXPERTS, dtype=jnp.int32)[None, None, :]
    marks = jnp.any(hits, axis=1)
    weight = jnp.sum(jnp.where(hits, gates[:, :, None], 0.0), axis=1)
    lower = (
        jnp.arange(rows, dtype=jnp.int32)[:, None] > jnp.arange(rows, dtype=jnp.int32)[None, :]
    ).astype(jnp.bfloat16)
    before = jnp.dot(lower, marks.astype(jnp.bfloat16), preferred_element_type=jnp.float32)
    slot = before.astype(jnp.int32)
    pick = marks[:, :, None] & (
        slot[:, :, None] == jnp.arange(capacity, dtype=jnp.int32)[None, None, :]
    )
    outgoing = jnp.einsum(
        "tec,tw->ecw", pick.astype(jnp.bfloat16), normed, preferred_element_type=jnp.float32
    ).astype(jnp.bfloat16)
    joined = lax.all_to_all(outgoing, ("req", "h"), split_axis=0, concat_axis=0, tiled=True)
    pieces = gate_up_all.reshape(gate_up_all.shape[0], slices, 2 * width_dev)
    gate_cols = pieces[..., :width_dev].reshape(gate_up_all.shape[0], slices * width_dev)
    up_cols = pieces[..., width_dev:].reshape(gate_up_all.shape[0], slices * width_dev)
    both = jnp.einsum(
        "scw,wh->sch",
        joined,
        jnp.concatenate([gate_cols, up_cols], axis=1),
        preferred_element_type=jnp.float32,
    )
    inner = slices * width_dev
    hidden = (jax.nn.silu(both[..., :inner]) * both[..., inner:]).astype(jnp.bfloat16)
    produced = jnp.einsum(
        "sch,hw->scw", hidden, down_all, preferred_element_type=jnp.float32
    ).astype(jnp.bfloat16)
    results = lax.all_to_all(produced, ("req", "h"), split_axis=0, concat_axis=0, tiled=True)
    scale = jnp.where(pick, weight[:, :, None], 0.0)
    mix = jnp.einsum(
        "tec,ecw->tw",
        scale,
        results.astype(jnp.float32),
        precision=lax.Precision.HIGHEST,
        preferred_element_type=jnp.float32,
    )
    return (branch.astype(jnp.bfloat16), mix.astype(jnp.bfloat16))


def solution(mesh):
    groups = mesh.shape["req"]
    slices = groups * mesh.shape["cuts"] // EXPERTS
    split = jax.sharding.Mesh(
        mesh.devices.reshape(groups, mesh.shape["cuts"] // slices, slices), ("req", "h", "q")
    )
    rows = ("req", "h", "q")
    placed = (
        P(rows, None),
        P(),
        P(),
        P(),
        P(),
        P(rows, None, None),
        P(rows, None, None),
        P(rows),
        P(rows, None),
        P(rows, None),
        P(rows, None, None),
        P(rows, None, None),
    )
    return jax.shard_map(
        on_device,
        mesh=split,
        in_specs=placed,
        out_specs=(P(rows, None), P(rows, None)),
        check_vma=False,
    )
```

```python
import jax
import jax.numpy as jnp
from jax import lax
from jax.sharding import PartitionSpec as P
from jax.experimental import pallas as pl
from jax.experimental.pallas import tpu as pltpu

HEADS = 16
KV_HEADS = 8
HEAD = 64
EXPERTS = 32
TOP = 8
CAPACITY = 40


def rms_scale(values, gain):
    wide = values.astype(jnp.float32)
    power = jnp.mean(wide * wide, axis=-1, keepdims=True)
    return wide * lax.rsqrt(power + 1e-06) * gain


def rotate(vectors, places):
    half = vectors.shape[-1] // 2
    freq = 10000.0 ** (-jnp.arange(half, dtype=jnp.float32) / half)
    angle = places[:, None] * freq[None, :]
    cosine = jnp.cos(angle)[:, None, :]
    sine = jnp.sin(angle)[:, None, :]
    first = vectors[..., :half]
    second = vectors[..., half:]
    return jnp.concatenate(
        [first * cosine - second * sine, second * cosine + first * sine], axis=-1
    )


def turn(values, cosine, sine, lead, half):
    partner = jnp.where(
        lead, pltpu.roll(values, values.shape[1] - half, 1), pltpu.roll(values, half, 1)
    )
    return jnp.where(lead, values * cosine - partner * sine, values * cosine + partner * sine)


def attention_kernel(length_ref, q_ref, k_ref, v_ref, cos_ref, sin_ref, kc_ref, vc_ref, o_ref):
    length = length_ref[0]
    span, lanes = kc_ref.shape
    rows = k_ref.shape[0]
    half = lanes // 2
    quarter = HEAD // 2
    cosine = cos_ref[...]
    sine = sin_ref[...]
    lane = lax.broadcasted_iota(jnp.int32, (rows, lanes), 1)
    lead = lane % HEAD < quarter
    low = lane < half
    kc = kc_ref[...]
    vc = vc_ref[...]
    kn = turn(k_ref[...], cosine, sine, lead, quarter).astype(jnp.bfloat16)
    vn = v_ref[...].astype(jnp.bfloat16)
    column = lax.broadcasted_iota(jnp.int32, (rows, span), 1)
    cache_ok = column < length
    new_col = lax.broadcasted_iota(jnp.int32, (rows, rows), 1)
    new_row = lax.broadcasted_iota(jnp.int32, (rows, rows), 0)
    new_ok = new_col <= new_row

    def scaled(values):
        rotated = turn(values, cosine, sine, lead, quarter).astype(jnp.bfloat16)
        return (rotated * 0.015625).astype(jnp.bfloat16).astype(jnp.float32)

    first = scaled(q_ref[:, :lanes])
    second = scaled(q_ref[:, lanes:])
    queries = (
        jnp.where(low, first, 0.0),
        jnp.where(low, pltpu.roll(first, half, 1), 0.0),
        jnp.where(low, 0.0, pltpu.roll(second, half, 1)),
        jnp.where(low, 0.0, second),
    )
    contract = (((1,), (1,)), ((), ()))
    outs = []
    for q in queries:
        q = q.astype(jnp.bfloat16)
        s = lax.dot_general(q, kc, contract, preferred_element_type=jnp.float32)
        s = jnp.where(cache_ok, s, -1e30)
        sn = lax.dot_general(q, kn, contract, preferred_element_type=jnp.float32)
        sn = jnp.where(new_ok, sn, -1e30)
        top = jnp.maximum(jnp.max(s, axis=1, keepdims=True), jnp.max(sn, axis=1, keepdims=True))
        e = jnp.exp(s - top)
        en = jnp.exp(sn - top)
        total = jnp.sum(e, axis=1, keepdims=True) + jnp.sum(en, axis=1, keepdims=True)
        inverse = 1.0 / total
        w = (e * inverse).astype(jnp.bfloat16)
        wn = (en * inverse).astype(jnp.bfloat16)
        o = jnp.dot(w, vc, preferred_element_type=jnp.float32) + jnp.dot(
            wn, vn, preferred_element_type=jnp.float32
        )
        o = o.astype(jnp.bfloat16).astype(jnp.float32)
        j = len(outs)
        outs.append(j)
        place = slice(0, lanes) if j < 2 else slice(lanes, 2 * lanes)
        if j % 2 == 0:
            o_ref[:, place] = o.astype(jnp.bfloat16)
        else:
            kept = o_ref[:, place].astype(jnp.float32)
            if j == 1:
                merged = jnp.where(low, kept, pltpu.roll(o, half, 1))
            else:
                merged = jnp.where(low, pltpu.roll(kept, half, 1), o)
            o_ref[:, place] = merged.astype(jnp.bfloat16)


def attention_core(length, mixed, cosine, sine, kc, vc, interpret=False):
    rows = mixed.shape[0]
    span, kvwidth = kc.shape
    qwidth = HEADS * HEAD
    lanes = 2 * HEAD
    pairs = kvwidth // lanes
    qblock = qwidth // pairs
    kstart = qwidth // lanes
    vstart = kstart + pairs
    return pl.pallas_call(
        attention_kernel,
        grid_spec=pltpu.PrefetchScalarGridSpec(
            num_scalar_prefetch=1,
            grid=(pairs,),
            in_specs=[
                pl.BlockSpec((rows, qblock), lambda p, n: (0, p)),
                pl.BlockSpec((rows, lanes), lambda p, n: (0, kstart + p)),
                pl.BlockSpec((rows, lanes), lambda p, n: (0, vstart + p)),
                pl.BlockSpec((rows, lanes), lambda p, n: (0, 0)),
                pl.BlockSpec((rows, lanes), lambda p, n: (0, 0)),
                pl.BlockSpec((span, lanes), lambda p, n: (0, p)),
                pl.BlockSpec((span, lanes), lambda p, n: (0, p)),
            ],
            out_specs=pl.BlockSpec((rows, qblock), lambda p, n: (0, p)),
        ),
        out_shape=jax.ShapeDtypeStruct((rows, qwidth), jnp.bfloat16),
        interpret=interpret,
    )(length, mixed, mixed, mixed, cosine, sine, kc, vc)


def attend(tokens, qkv_weight, out_weight, norm_attn, keys_cache, values_cache, length, interpret=False):
    rows = tokens.shape[0]
    half = HEAD // 2
    normed = rms_scale(tokens, norm_attn).astype(jnp.bfloat16)
    mixed = jnp.dot(normed, qkv_weight, preferred_element_type=jnp.float32)
    places = (length + jnp.arange(rows, dtype=jnp.int32)).astype(jnp.float32)
    index = (jnp.arange(2 * HEAD, dtype=jnp.int32) % half).astype(jnp.float32)
    freq = 10000.0 ** (-index / half)
    angle = places[:, None] * freq[None, :]
    cosine = jnp.cos(angle)
    sine = jnp.sin(angle)
    heads_out = attention_core(
        length.reshape(1).astype(jnp.int32),
        mixed,
        cosine,
        sine,
        keys_cache,
        values_cache,
        interpret=interpret,
    )
    return jnp.dot(heads_out, out_weight, preferred_element_type=jnp.float32)


def swap(piece, bit):
    return lax.ppermute(piece, "q", [(i, i ^ bit) for i in range(lax.axis_size("q"))])


def on_device(
    tokens,
    qkv_weight,
    out_weight,
    norm_attn,
    norm_expert,
    keys_cache,
    values_cache,
    lengths,
    routes,
    gates,
    gate_up,
    down_weight,
):
    slices = lax.axis_size("q")
    width_dev = down_weight.shape[1]
    own_gu = gate_up[0]
    own_dw = down_weight[0]
    far_gu = swap(own_gu, 2)
    far_dw = swap(own_dw, 2)
    side_gu = swap(own_gu, 1)
    side_dw = swap(own_dw, 1)
    branch = attend(
        tokens, qkv_weight, out_weight, norm_attn, keys_cache[0], values_cache[0], lengths[0]
    )
    branch, far_gu, far_dw = lax.optimization_barrier((branch, far_gu, far_dw))
    gate_up_all = jnp.concatenate([own_gu, far_gu, side_gu, swap(far_gu, 1)], axis=1)
    down_all = jnp.concatenate([own_dw, far_dw, side_dw, swap(far_dw, 1)], axis=0)
    carried = tokens.astype(jnp.float32) + 0.22 * branch
    normed = rms_scale(carried, norm_expert).astype(jnp.bfloat16)
    rows, width = normed.shape
    capacity = CAPACITY
    hits = routes[:, :, None] == jnp.arange(EXPERTS, dtype=jnp.int32)[None, None, :]
    marks = jnp.any(hits, axis=1)
    weight = jnp.sum(jnp.where(hits, gates[:, :, None], 0.0), axis=1)
    lower = (
        jnp.arange(rows, dtype=jnp.int32)[:, None] > jnp.arange(rows, dtype=jnp.int32)[None, :]
    ).astype(jnp.bfloat16)
    before = jnp.dot(lower, marks.astype(jnp.bfloat16), preferred_element_type=jnp.float32)
    slot = before.astype(jnp.int32)
    pick = marks[:, :, None] & (
        slot[:, :, None] == jnp.arange(capacity, dtype=jnp.int32)[None, None, :]
    )
    outgoing = jnp.einsum(
        "tec,tw->ecw", pick.astype(jnp.bfloat16), normed, preferred_element_type=jnp.float32
    ).astype(jnp.bfloat16)
    joined = lax.all_to_all(outgoing, ("req", "h"), split_axis=0, concat_axis=0, tiled=True)
    pieces = gate_up_all.reshape(gate_up_all.shape[0], slices, 2 * width_dev)
    gate_cols = pieces[..., :width_dev].reshape(gate_up_all.shape[0], slices * width_dev)
    up_cols = pieces[..., width_dev:].reshape(gate_up_all.shape[0], slices * width_dev)
    both = jnp.einsum(
        "scw,wh->sch",
        joined,
        jnp.concatenate([gate_cols, up_cols], axis=1),
        preferred_element_type=jnp.float32,
    )
    inner = slices * width_dev
    hidden = (jax.nn.silu(both[..., :inner]) * both[..., inner:]).astype(jnp.bfloat16)
    produced = jnp.einsum(
        "sch,hw->scw", hidden, down_all, preferred_element_type=jnp.float32
    ).astype(jnp.bfloat16)
    results = lax.all_to_all(produced, ("req", "h"), split_axis=0, concat_axis=0, tiled=True)
    scale = jnp.where(pick, weight[:, :, None], 0.0)
    mix = jnp.einsum(
        "tec,ecw->tw",
        scale,
        results.astype(jnp.float32),
        precision=lax.Precision.HIGH,
        preferred_element_type=jnp.float32,
    )
    return (branch.astype(jnp.bfloat16), mix.astype(jnp.bfloat16))


def solution(mesh):
    groups = mesh.shape["req"]
    slices = groups * mesh.shape["cuts"] // EXPERTS
    split = jax.sharding.Mesh(
        mesh.devices.reshape(groups, mesh.shape["cuts"] // slices, slices), ("req", "h", "q")
    )
    rows = ("req", "h", "q")
    placed = (
        P(rows, None),
        P(),
        P(),
        P(),
        P(),
        P(rows, None, None),
        P(rows, None, None),
        P(rows),
        P(rows, None),
        P(rows, None),
        P(rows, None, None),
        P(rows, None, None),
    )
    return jax.shard_map(
        on_device,
        mesh=split,
        in_specs=placed,
        out_specs=(P(rows, None), P(rows, None)),
        check_vma=False,
    )
```

```python
import jax
import jax.numpy as jnp
from jax import lax
from jax.sharding import PartitionSpec as P
from jax.experimental import pallas as pl
from jax.experimental.pallas import tpu as pltpu

HEADS = 16
KV_HEADS = 8
HEAD = 64
EXPERTS = 32
TOP = 8
CAPACITY = 40


def rms_scale(values, gain):
    wide = values.astype(jnp.float32)
    power = jnp.mean(wide * wide, axis=-1, keepdims=True)
    return wide * lax.rsqrt(power + 1e-06) * gain


def rotate(vectors, places):
    half = vectors.shape[-1] // 2
    freq = 10000.0 ** (-jnp.arange(half, dtype=jnp.float32) / half)
    angle = places[:, None] * freq[None, :]
    cosine = jnp.cos(angle)[:, None, :]
    sine = jnp.sin(angle)[:, None, :]
    first = vectors[..., :half]
    second = vectors[..., half:]
    return jnp.concatenate(
        [first * cosine - second * sine, second * cosine + first * sine], axis=-1
    )


def turn(values, cosine, sine, lead, half):
    partner = jnp.where(
        lead, pltpu.roll(values, values.shape[1] - half, 1), pltpu.roll(values, half, 1)
    )
    return jnp.where(lead, values * cosine - partner * sine, values * cosine + partner * sine)


def attention_kernel(length_ref, q_ref, k_ref, v_ref, cos_ref, sin_ref, kc_ref, vc_ref, o_ref):
    length = length_ref[0]
    span, lanes = kc_ref.shape
    rows = k_ref.shape[0]
    half = lanes // 2
    quarter = HEAD // 2
    cosine = cos_ref[...]
    sine = sin_ref[...]
    lane = lax.broadcasted_iota(jnp.int32, (rows, lanes), 1)
    lead = lane % HEAD < quarter
    low = lane < half
    kc = kc_ref[...]
    vc = vc_ref[...]
    kn = turn(k_ref[...], cosine, sine, lead, quarter).astype(jnp.bfloat16)
    vn = v_ref[...].astype(jnp.bfloat16)
    column = lax.broadcasted_iota(jnp.int32, (rows, span), 1)
    cache_ok = column < length
    new_col = lax.broadcasted_iota(jnp.int32, (rows, rows), 1)
    new_row = lax.broadcasted_iota(jnp.int32, (rows, rows), 0)
    new_ok = new_col <= new_row

    def scaled(values):
        rotated = turn(values, cosine, sine, lead, quarter).astype(jnp.bfloat16)
        return (rotated * 0.015625).astype(jnp.bfloat16).astype(jnp.float32)

    first = scaled(q_ref[:, :lanes])
    second = scaled(q_ref[:, lanes:])
    queries = (
        jnp.where(low, first, 0.0),
        jnp.where(low, pltpu.roll(first, half, 1), 0.0),
        jnp.where(low, 0.0, pltpu.roll(second, half, 1)),
        jnp.where(low, 0.0, second),
    )
    contract = (((1,), (1,)), ((), ()))
    outs = []
    for q in queries:
        q = q.astype(jnp.bfloat16)
        s = lax.dot_general(q, kc, contract, preferred_element_type=jnp.float32)
        s = jnp.where(cache_ok, s, -1e30)
        sn = lax.dot_general(q, kn, contract, preferred_element_type=jnp.float32)
        sn = jnp.where(new_ok, sn, -1e30)
        top = jnp.maximum(jnp.max(s, axis=1, keepdims=True), jnp.max(sn, axis=1, keepdims=True))
        e = jnp.exp(s - top)
        en = jnp.exp(sn - top)
        total = jnp.sum(e, axis=1, keepdims=True) + jnp.sum(en, axis=1, keepdims=True)
        inverse = 1.0 / total
        w = (e * inverse).astype(jnp.bfloat16)
        wn = (en * inverse).astype(jnp.bfloat16)
        o = jnp.dot(w, vc, preferred_element_type=jnp.float32) + jnp.dot(
            wn, vn, preferred_element_type=jnp.float32
        )
        o = o.astype(jnp.bfloat16).astype(jnp.float32)
        j = len(outs)
        outs.append(j)
        place = slice(0, lanes) if j < 2 else slice(lanes, 2 * lanes)
        if j % 2 == 0:
            o_ref[:, place] = o.astype(jnp.bfloat16)
        else:
            kept = o_ref[:, place].astype(jnp.float32)
            if j == 1:
                merged = jnp.where(low, kept, pltpu.roll(o, half, 1))
            else:
                merged = jnp.where(low, pltpu.roll(kept, half, 1), o)
            o_ref[:, place] = merged.astype(jnp.bfloat16)


def attention_core(length, mixed, cosine, sine, kc, vc, interpret=False):
    rows = mixed.shape[0]
    span, kvwidth = kc.shape
    qwidth = HEADS * HEAD
    lanes = 2 * HEAD
    pairs = kvwidth // lanes
    qblock = qwidth // pairs
    kstart = qwidth // lanes
    vstart = kstart + pairs
    return pl.pallas_call(
        attention_kernel,
        grid_spec=pltpu.PrefetchScalarGridSpec(
            num_scalar_prefetch=1,
            grid=(pairs,),
            in_specs=[
                pl.BlockSpec((rows, qblock), lambda p, n: (0, p)),
                pl.BlockSpec((rows, lanes), lambda p, n: (0, kstart + p)),
                pl.BlockSpec((rows, lanes), lambda p, n: (0, vstart + p)),
                pl.BlockSpec((rows, lanes), lambda p, n: (0, 0)),
                pl.BlockSpec((rows, lanes), lambda p, n: (0, 0)),
                pl.BlockSpec((span, lanes), lambda p, n: (0, p)),
                pl.BlockSpec((span, lanes), lambda p, n: (0, p)),
            ],
            out_specs=pl.BlockSpec((rows, qblock), lambda p, n: (0, p)),
        ),
        out_shape=jax.ShapeDtypeStruct((rows, qwidth), jnp.bfloat16),
        interpret=interpret,
    )(length, mixed, mixed, mixed, cosine, sine, kc, vc)


def attend(tokens, qkv_weight, out_weight, norm_attn, keys_cache, values_cache, length, interpret=False):
    rows = tokens.shape[0]
    half = HEAD // 2
    normed = rms_scale(tokens, norm_attn).astype(jnp.bfloat16)
    mixed = jnp.dot(normed, qkv_weight, preferred_element_type=jnp.float32)
    places = (length + jnp.arange(rows, dtype=jnp.int32)).astype(jnp.float32)
    index = (jnp.arange(2 * HEAD, dtype=jnp.int32) % half).astype(jnp.float32)
    freq = 10000.0 ** (-index / half)
    angle = places[:, None] * freq[None, :]
    cosine = jnp.cos(angle)
    sine = jnp.sin(angle)
    heads_out = attention_core(
        length.reshape(1).astype(jnp.int32),
        mixed,
        cosine,
        sine,
        keys_cache,
        values_cache,
        interpret=interpret,
    )
    return jnp.dot(heads_out, out_weight, preferred_element_type=jnp.float32)


def swap(piece, bit):
    return lax.ppermute(piece, "q", [(i, i ^ bit) for i in range(lax.axis_size("q"))])


def on_device(
    tokens,
    qkv_weight,
    out_weight,
    norm_attn,
    norm_expert,
    keys_cache,
    values_cache,
    lengths,
    routes,
    gates,
    gate_up,
    down_weight,
):
    slices = lax.axis_size("q")
    width_dev = down_weight.shape[1]
    own_gu = gate_up[0]
    own_dw = down_weight[0]
    far_gu = swap(own_gu, 2)
    far_dw = swap(own_dw, 2)
    branch = attend(
        tokens, qkv_weight, out_weight, norm_attn, keys_cache[0], values_cache[0], lengths[0]
    )
    branch, far_gu, far_dw, own_gu, own_dw = lax.optimization_barrier(
        (branch, far_gu, far_dw, own_gu, own_dw)
    )
    side_gu = swap(own_gu, 1)
    side_dw = swap(own_dw, 1)
    gate_up_all = jnp.concatenate([own_gu, far_gu, side_gu, swap(far_gu, 1)], axis=1)
    down_all = jnp.concatenate([own_dw, far_dw, side_dw, swap(far_dw, 1)], axis=0)
    carried = tokens.astype(jnp.float32) + 0.22 * branch
    normed = rms_scale(carried, norm_expert).astype(jnp.bfloat16)
    rows, width = normed.shape
    capacity = CAPACITY
    hits = routes[:, :, None] == jnp.arange(EXPERTS, dtype=jnp.int32)[None, None, :]
    marks = jnp.any(hits, axis=1)
    weight = jnp.sum(jnp.where(hits, gates[:, :, None], 0.0), axis=1)
    lower = (
        jnp.arange(rows, dtype=jnp.int32)[:, None] > jnp.arange(rows, dtype=jnp.int32)[None, :]
    ).astype(jnp.bfloat16)
    before = jnp.dot(lower, marks.astype(jnp.bfloat16), preferred_element_type=jnp.float32)
    slot = before.astype(jnp.int32)
    pick = marks[:, :, None] & (
        slot[:, :, None] == jnp.arange(capacity, dtype=jnp.int32)[None, None, :]
    )
    outgoing = jnp.einsum(
        "tec,tw->ecw", pick.astype(jnp.bfloat16), normed, preferred_element_type=jnp.float32
    ).astype(jnp.bfloat16)
    joined = lax.all_to_all(outgoing, ("req", "h"), split_axis=0, concat_axis=0, tiled=True)
    pieces = gate_up_all.reshape(gate_up_all.shape[0], slices, 2 * width_dev)
    gate_cols = pieces[..., :width_dev].reshape(gate_up_all.shape[0], slices * width_dev)
    up_cols = pieces[..., width_dev:].reshape(gate_up_all.shape[0], slices * width_dev)
    both = jnp.einsum(
        "scw,wh->sch",
        joined,
        jnp.concatenate([gate_cols, up_cols], axis=1),
        preferred_element_type=jnp.float32,
    )
    inner = slices * width_dev
    hidden = (jax.nn.silu(both[..., :inner]) * both[..., inner:]).astype(jnp.bfloat16)
    produced = jnp.einsum(
        "sch,hw->scw", hidden, down_all, preferred_element_type=jnp.float32
    ).astype(jnp.bfloat16)
    results = lax.all_to_all(produced, ("req", "h"), split_axis=0, concat_axis=0, tiled=True)
    scale = jnp.where(pick, weight[:, :, None], 0.0)
    mix = jnp.einsum(
        "tec,ecw->tw",
        scale,
        results.astype(jnp.float32),
        precision=lax.Precision.HIGH,
        preferred_element_type=jnp.float32,
    )
    return (branch.astype(jnp.bfloat16), mix.astype(jnp.bfloat16))


def solution(mesh):
    groups = mesh.shape["req"]
    slices = groups * mesh.shape["cuts"] // EXPERTS
    split = jax.sharding.Mesh(
        mesh.devices.reshape(groups, mesh.shape["cuts"] // slices, slices), ("req", "h", "q")
    )
    rows = ("req", "h", "q")
    placed = (
        P(rows, None),
        P(),
        P(),
        P(),
        P(),
        P(rows, None, None),
        P(rows, None, None),
        P(rows),
        P(rows, None),
        P(rows, None),
        P(rows, None, None),
        P(rows, None, None),
    )
    return jax.shard_map(
        on_device,
        mesh=split,
        in_specs=placed,
        out_specs=(P(rows, None), P(rows, None)),
        check_vma=False,
    )
```
